1024 devices in a mesh: along: 64 (over z, x), across: 16 (over y, core).
Axes of the slice: x: 8, y: 8, z: 8, core: 2. Of those that a mesh axis runs over, the one named last changes fastest.
Arguments:
- features: bfloat16 [1048576, 256], P(('along', 'across')), may hold values from -6 to 6
- adj_tiles: bfloat16 [8192, 4, 128, 128], P(('along', 'across')), may hold values from -0.25 to 0.25
- adj_index: int32 [8192, 4], P(('along', 'across')), may hold values from 0 to 11, as said below
- adj_count: int32 [8192], P(('along', 'across')), may hold values from 2 to 4, as said below
- bnd_index: int32 [131072], P(('along', 'across')), may hold values from 0 to 1023
- pool_index: int32 [1048576], P(('along', 'across')), may hold values from 0 to 63
- w_msg: bfloat16 [256, 256], replicated, may hold values from -0.375 to 0.375
- w_update: bfloat16 [512, 256], replicated, may hold values from -0.25 to 0.25
- w_coarse: bfloat16 [256, 256], replicated, may hold values from -0.375 to 0.375
- cotangent: bfloat16 [1048576, 256], P(('along', 'across')), may hold values from -0.125 to 0.125
Outputs:
- updated: bfloat16 [1048576, 256], P(('along', 'across'))
- weight_grads: float32 [131072], P(('along', 'across'))
The draws below stay inside these ranges and needn't reach their ends.
Inputs may be any that keep to these rules, and one draw needn't show every extreme that they name: `adj_index`: indices 0 to 7 name the partition's own blocks, 8 to 11 the four boundary tiles in the order of the sources. Slot 0 of every block names the block itself. Slots from adj_count on are ignored. Some block has all 4 slots live.
All inputs are finite; a program needn't handle non-finite values.
Results may differ from the reference program's by a relative error of at most 0.0062.
Values may be sent and summed in bfloat16 or wider, within the bound.
No kernel may reach another device: no remote copies, remote signals or barrier semaphores. Data moves between devices by JAX's collectives and lax.ppermute only.
A program may use at most 32 MiB of HBM per device.

```python
import jax
import jax.numpy as jnp
from jax import lax

H = 256
TILE = 128
BLK_DEV = 8
KT = 4
NODE_DEV = 1024
NODES = 1048576
NBLK = 8192
NCS = 64
N_ALONG = 64
N_ACROSS = 16


def draw_adj_index(key, part):
    first_key, second_key = jax.random.split(jax.random.fold_in(key, 11))
    block_ids = jnp.arange(NBLK, dtype=jnp.int32)
    local_block = block_ids % BLK_DEV
    owner = block_ids // BLK_DEV
    turn = jax.random.randint(first_key, (NBLK // BLK_DEV,), 0, 4, dtype=jnp.int32)
    side = BLK_DEV + (local_block + turn[owner]) % 4
    others = jax.random.randint(second_key, (NBLK, KT - 2), 0, BLK_DEV + 4, dtype=jnp.int32)
    return jnp.concatenate([local_block[:, None], side[:, None], others], axis=1).astype(jnp.int32)


def draw_adj_count(key, part):
    first_key, second_key = jax.random.split(jax.random.fold_in(key, 23))
    level = jax.random.randint(first_key, (NBLK // BLK_DEV,), 2, KT + 1, dtype=jnp.int32)
    jitter = jax.random.randint(second_key, (NBLK,), -1, 2, dtype=jnp.int32)
    owner = jnp.arange(NBLK, dtype=jnp.int32) // BLK_DEV
    counts = jnp.clip(level[owner] + jitter, 2, KT)
    return counts.at[0].set(KT).astype(jnp.int32)


def with_ends(values, rng, least, high):
    extent = values.shape
    spot = [jax.random.randint(jax.random.fold_in(rng, axis), (), 0, extent[axis]) for axis in range(len(extent))]
    values = values.at[tuple(spot)].set(least)
    longest = extent.index(max(extent))
    spot[longest] = (spot[longest] + 1) % extent[longest]
    return values.at[tuple(spot)].set(high)


def strengthened(values, key, source, target, parts, factor):
    owner, partner = [(jnp.arange(values.shape[position]) // (values.shape[position] // parts)).reshape([-1 if axis == position else 1 for axis in range(values.ndim)]) for position in (source, target)]
    chosen = jax.random.permutation(key, parts)[partner]
    strong = (owner == chosen) | (owner == (partner + parts // 2) % parts)
    return jnp.where(strong, factor * values, values)


def block_scale(own_key, dims, shards, least, high):
    def one(dim, parts):
        steps = jax.random.uniform(jax.random.fold_in(jax.random.fold_in(own_key, 6), dim), (parts,), jnp.float32, least / len(shards), high / len(shards))
        return jnp.repeat(jnp.exp(steps), dims[dim] // parts).reshape((-1,) + (1,) * (len(dims) - dim - 1))

    loudness = one(*shards[0])
    for cut in shards[1:]:
        loudness = loudness * one(*cut)
    return loudness


def scatter_about(stream_key, dims, deviation, bound, shards=(), kind=jnp.bfloat16):
    values = deviation * jax.random.normal(stream_key, dims, jnp.float32)
    if shards:
        values = values * block_scale(stream_key, dims, shards, -0.22, 0.18)
    return jnp.clip(values, -bound, bound).astype(kind)


def bell_draw_with(stream_key, extent, width, bound, shards, heavy, kind=jnp.bfloat16):
    drawn = width * jax.random.normal(stream_key, extent, jnp.float32)
    if shards:
        drawn = drawn * block_scale(stream_key, extent, shards, -0.22, 0.18)
    return jnp.clip(strengthened(drawn, jax.random.fold_in(stream_key, 3), *heavy), -bound, bound).astype(kind)


def setup_inputs(seed: int = 0) -> dict:
    key_of = jax.random.split(jax.random.key(seed), 11)
    return {
        "features": scatter_about(key_of[0], (NODES, H), 1.0, 6.0, ((0, 1024),)),
        "adj_tiles": scatter_about(key_of[1], (NBLK, KT, TILE, TILE), (KT * TILE) ** -0.5, 0.25, ((0, 1024),)),
        "adj_index": draw_adj_index(jax.random.fold_in(key_of[10], 71), 0),
        "adj_count": draw_adj_count(jax.random.fold_in(key_of[10], 71), 0),
        "bnd_index": with_ends(jax.random.randint(key_of[4], (N_ALONG * N_ACROSS * TILE,), 0, NODE_DEV), jax.random.fold_in(key_of[4], 1), 0, NODE_DEV - 1).astype(jnp.int32),
        "pool_index": with_ends(jax.random.randint(key_of[5], (NODES,), 0, NCS), jax.random.fold_in(key_of[5], 1), 0, NCS - 1).astype(jnp.int32),
        "w_msg": scatter_about(key_of[6], (H, H), H ** -0.5, 0.375),
        "w_update": scatter_about(key_of[7], (2 * H, H), (2 * H) ** -0.5, 0.25),
        "w_coarse": scatter_about(key_of[8], (H, H), H ** -0.5, 0.375),
        "cotangent": bell_draw_with(key_of[9], (NODES, H), (2.0 * NODES ** -0.5), 0.125, ((0, 1024),), (0, 1, 256, 6.0)),
    }


eps = 1e-05

def normalize(values):
    center = values - lax.optimization_barrier(jnp.mean(values, axis=-1, keepdims=True))
    inverse = lax.rsqrt(lax.optimization_barrier(jnp.mean(center * center, axis=-1, keepdims=True)) + eps)
    return (center * inverse, inverse)

def silu_slope(values):
    logistic = jax.nn.sigmoid(values)
    return logistic * (1.0 + values * (1.0 - logistic))

def pick_rows(matrix_rows, row_index):
    return matrix_rows[row_index]

def reference(features, adj_tiles, adj_index, adj_count, bnd_index, pool_index, w_msg, w_update, w_coarse, cotangent):
    devices = N_ALONG * N_ACROSS
    node_dev = BLK_DEV * TILE
    inputs = features.astype(jnp.float32)
    normed, _ = normalize(inputs)
    scaled = normed.astype(jnp.bfloat16)
    local_rows = scaled.reshape(devices, node_dev, H)
    rim_index = bnd_index.reshape(devices, TILE)
    rim_rows = jax.vmap(pick_rows)(local_rows, rim_index)
    rim_grid = rim_rows.reshape(N_ALONG, N_ACROSS, TILE, H)
    padded = jnp.pad(rim_grid, ((1, 1), (1, 1), (0, 0), (0, 0)))
    halo_tiles = jnp.stack([padded[:-2, 1:-1], padded[2:, 1:-1], padded[1:-1, :-2], padded[1:-1, 2:]], axis=2)
    halo_tiles = halo_tiles.reshape(devices, 4, TILE, H)
    sources = jnp.concatenate([local_rows.reshape(devices, BLK_DEV, TILE, H), halo_tiles], axis=1)
    messages = jnp.dot(sources.reshape(-1, H), w_msg, preferred_element_type=jnp.float32)
    messages = messages.astype(jnp.bfloat16).reshape(sources.shape)
    live_slots = jnp.arange(KT)[None, :] < adj_count[:, None]
    tiles_dev = adj_tiles.reshape(devices, BLK_DEV, KT, TILE, TILE)
    index_dev = adj_index.reshape(devices, BLK_DEV, KT)
    live_dev = live_slots.reshape(devices, BLK_DEV, KT)

    def aggregate(operands):
        tile_set, index_set, live_set, message_set, source_set = operands
        weights = jnp.where(live_set[:, :, None, None], tile_set.astype(jnp.float32), jnp.zeros((), jnp.float32))
        first = jnp.einsum('bkij,bkjh->bih', weights, message_set[index_set].astype(jnp.float32), precision=lax.Precision.HIGHEST)
        second = jnp.einsum('bkij,bkjh->bih', weights, source_set[index_set].astype(jnp.float32), precision=lax.Precision.HIGHEST)
        return (first.astype(jnp.bfloat16), second.astype(jnp.bfloat16))
    aggregated, summed_scaled = lax.map(aggregate, (tiles_dev, index_dev, live_dev, messages, sources))
    aggregated = aggregated.reshape(NODES, H)
    summed_scaled = summed_scaled.reshape(NODES, H)
    joined = jnp.concatenate([scaled, aggregated], axis=1)
    update_pre = jnp.dot(joined, w_update, preferred_element_type=jnp.float32)
    hidden_one = inputs + jax.nn.silu(update_pre)
    segment_ids = (jnp.arange(NODES) // node_dev // N_ACROSS * NCS).astype(jnp.int32) + pool_index.astype(jnp.int32)
    pooled = jax.ops.segment_sum(hidden_one, segment_ids, num_segments=N_ALONG * NCS)
    coarse_norm, inverse = normalize(pooled)
    coarse = coarse_norm.astype(jnp.bfloat16)
    coarse_pre = jnp.dot(coarse, w_coarse, preferred_element_type=jnp.float32)
    coarse_out = jax.nn.silu(coarse_pre).astype(jnp.bfloat16)
    hidden_two = hidden_one + coarse_out[segment_ids].astype(jnp.float32)
    cot_float = cotangent.astype(jnp.float32)
    coarse_cot = jax.ops.segment_sum(cot_float, segment_ids, num_segments=N_ALONG * NCS)
    coarse_delta = (coarse_cot * silu_slope(coarse_pre)).astype(jnp.bfloat16)
    coarse_grad = jnp.dot(coarse.T, coarse_delta, preferred_element_type=jnp.float32)
    coarse_back = jnp.dot(coarse_delta, w_coarse.T, preferred_element_type=jnp.float32)
    mean_one = lax.optimization_barrier(jnp.mean(coarse_back, axis=-1, keepdims=True))
    mean_two = lax.optimization_barrier(jnp.mean(coarse_back * coarse_norm, axis=-1, keepdims=True))
    pooled_delta = inverse * (coarse_back - mean_one - coarse_norm * mean_two)
    hidden_delta = cot_float + pooled_delta[segment_ids]
    update_delta = (hidden_delta * silu_slope(update_pre)).astype(jnp.bfloat16)
    aggregated_delta = jnp.dot(update_delta, w_update[H:].T, preferred_element_type=jnp.float32).astype(jnp.bfloat16)
    message_grad = jnp.dot(summed_scaled.T, aggregated_delta, preferred_element_type=jnp.float32)
    weight_grads = jnp.concatenate([message_grad.reshape(-1), coarse_grad.reshape(-1)])
    return (hidden_two.astype(jnp.bfloat16), weight_grads)
```

```python
import jax
import jax.numpy as jnp
from jax import lax
from jax.sharding import PartitionSpec as P

NC_DEV = 4


eps = 1e-05


def partner_pairs(count, distance):
    return [(i, i ^ distance) for i in range(count)]


def butterfly_sum(values, axis):
    count = lax.axis_size(axis)
    distance = 1
    while distance < count:
        values = values + lax.ppermute(values, axis, partner_pairs(count, distance))
        distance *= 2
    return values


def halving_scatter(values, axes):
    steps = []
    for axis in reversed(axes):
        count = lax.axis_size(axis)
        distance = 1
        while distance < count:
            steps.append((axis, count, distance))
            distance *= 2
    chunk = values.shape[0] // (1 << len(steps))
    values = values.reshape(-1, chunk)
    for axis, count, distance in steps:
        bit = (lax.axis_index(axis) // distance) % 2
        pairs = values.reshape(-1, 2, chunk)
        keep = jnp.where(bit == 0, pairs[:, 0], pairs[:, 1])
        send = jnp.where(bit == 0, pairs[:, 1], pairs[:, 0])
        values = keep + lax.ppermute(send, axis, partner_pairs(count, distance))
    return values.reshape(-1)


def neighbour_tiles(tile):
    tiles = []
    for axis in ("along", "across"):
        count = lax.axis_size(axis)
        forward = [(i, i + 1) for i in range(count - 1)]
        backward = [(i + 1, i) for i in range(count - 1)]
        tiles.append(lax.ppermute(tile, axis, forward))
        tiles.append(lax.ppermute(tile, axis, backward))
    return jnp.stack(tiles)


def normalize(values):
    center = values - jnp.mean(values, axis=-1, keepdims=True)
    inverse = lax.rsqrt(jnp.mean(center * center, axis=-1, keepdims=True) + eps)
    return (center * inverse, inverse)


def silu_slope(values):
    logistic = jax.nn.sigmoid(values)
    return logistic * (1.0 + values * (1.0 - logistic))


def transposed_times(operand, second, precision=None):
    return lax.dot_general(
        operand,
        second,
        (((0,), (0,)), ((), ())),
        precision=precision,
        preferred_element_type=jnp.float32,
    )


def times_transposed(operand, second):
    return lax.dot_general(
        operand, second, (((1,), (1,)), ((), ())), preferred_element_type=jnp.float32
    )


def coarse_forward(pooled, w_coarse):
    coarse_norm, inverse = normalize(pooled)
    coarse = coarse_norm.astype(jnp.bfloat16)
    coarse_pre = jnp.dot(coarse, w_coarse, preferred_element_type=jnp.float32)
    return (coarse_norm, inverse, coarse, coarse_pre, jax.nn.silu(coarse_pre).astype(jnp.bfloat16))


def coarse_backward(coarse_cot, coarse_norm, inverse, coarse_pre, w_coarse):
    coarse_delta = (coarse_cot * silu_slope(coarse_pre)).astype(jnp.bfloat16)
    coarse_back = times_transposed(coarse_delta, w_coarse)
    mean_one = jnp.mean(coarse_back, axis=-1, keepdims=True)
    mean_two = jnp.mean(coarse_back * coarse_norm, axis=-1, keepdims=True)
    return (coarse_delta, inverse * (coarse_back - mean_one - coarse_norm * mean_two))


def local(
    features,
    adj_tiles,
    adj_index,
    adj_count,
    bnd_index,
    pool_index,
    w_msg,
    w_update,
    w_coarse,
    cotangent,
):
    feature_count = features.shape[1]
    blocks = adj_tiles.shape[0]
    slot_count = adj_tiles.shape[1]
    tile_rows = adj_tiles.shape[2]
    inputs = features.astype(jnp.float32)
    normed, _ = normalize(inputs)
    scaled = normed.astype(jnp.bfloat16)
    rim_rows = scaled[bnd_index]
    halo_tiles = neighbour_tiles(rim_rows)
    sources = jnp.concatenate(
        [scaled.reshape(blocks, tile_rows, feature_count), halo_tiles], axis=0
    )
    messages = jnp.dot(
        sources.reshape(-1, feature_count), w_msg, preferred_element_type=jnp.float32
    )
    messages = messages.astype(jnp.bfloat16).reshape(sources.shape)
    live_slots = jnp.arange(slot_count)[None, :] < adj_count[:, None]
    masked_tiles = jnp.where(live_slots[:, :, None, None], adj_tiles, jnp.zeros((), jnp.bfloat16))
    aggregated = jnp.einsum(
        "bkij,bkjh->bih", masked_tiles, messages[adj_index], preferred_element_type=jnp.float32
    )
    aggregated = aggregated.astype(jnp.bfloat16).reshape(-1, feature_count)
    summed_scaled = jnp.einsum(
        "bkij,bkjh->bih", masked_tiles, sources[adj_index], preferred_element_type=jnp.float32
    )
    summed_scaled = summed_scaled.astype(jnp.bfloat16).reshape(-1, feature_count)
    w_first = w_update[:feature_count]
    w_second = w_update[feature_count:]
    update_pre = jnp.dot(scaled, w_first, preferred_element_type=jnp.float32) + jnp.dot(
        aggregated, w_second, preferred_element_type=jnp.float32
    )
    hidden_one = inputs + jax.nn.silu(update_pre)
    coarse_count = NC_DEV * lax.axis_size("across")
    assign_float = (pool_index[:, None] == jnp.arange(coarse_count)[None, :]).astype(jnp.float32)
    assign_bits = assign_float.astype(jnp.bfloat16)
    pooled_part = transposed_times(assign_float, hidden_one, lax.Precision.HIGHEST)
    cot_part = transposed_times(assign_bits, cotangent)
    pooled, coarse_cot = butterfly_sum(jnp.stack([pooled_part, cot_part]), "across")
    coarse_norm, inverse, coarse, coarse_pre, coarse_out = coarse_forward(pooled, w_coarse)
    hidden_two = hidden_one + jnp.dot(assign_bits, coarse_out, preferred_element_type=jnp.float32)
    coarse_delta, pooled_delta = coarse_backward(
        coarse_cot, coarse_norm, inverse, coarse_pre, w_coarse
    )
    start = lax.axis_index("across") * NC_DEV
    own_coarse = lax.dynamic_slice_in_dim(coarse, start, NC_DEV, 0)
    own_coarse_delta = lax.dynamic_slice_in_dim(coarse_delta, start, NC_DEV, 0)
    coarse_grad = transposed_times(own_coarse, own_coarse_delta)
    hidden_delta = cotangent.astype(jnp.float32) + jnp.dot(
        assign_float,
        pooled_delta,
        precision=lax.Precision.HIGHEST,
        preferred_element_type=jnp.float32,
    )
    update_delta = (hidden_delta * silu_slope(update_pre)).astype(jnp.bfloat16)
    aggregated_delta = times_transposed(update_delta, w_second).astype(jnp.bfloat16)
    message_grad = transposed_times(summed_scaled, aggregated_delta)
    grad_terms = jnp.concatenate([message_grad.reshape(-1), coarse_grad.reshape(-1)])
    weight_grads = halving_scatter(grad_terms, ("along", "across"))
    return (hidden_two.astype(jnp.bfloat16), weight_grads)


def solution(mesh):
    return jax.shard_map(
        local,
        mesh=mesh,
        in_specs=(
            P(("along", "across"), None),
            P(("along", "across"), None, None, None),
            P(("along", "across"), None),
            P(("along", "across")),
            P(("along", "across")),
            P(("along", "across")),
            P(),
            P(),
            P(),
            P(("along", "across"), None),
        ),
        out_specs=(P(("along", "across"), None), P(("along", "across"))),
        check_vma=False,
    )
```

```python
import jax
import jax.numpy as jnp
from jax import lax
from jax.sharding import PartitionSpec as P

NC_DEV = 4


eps = 1e-05


def scatter_sum(pieces, axes):
    return lax.all_to_all(pieces, axes, 0, 0, tiled=False).sum(0)


def all_sum(values, axis):
    count = lax.axis_size(axis)
    mine = scatter_sum(values.reshape(count, -1), axis)
    gathered = lax.all_to_all(jnp.broadcast_to(mine, (count,) + mine.shape), axis, 0, 0, tiled=False)
    return gathered.reshape(values.shape)


def neighbour_tiles(tile):
    tiles = []
    for axis in ("along", "across"):
        count = lax.axis_size(axis)
        forward = [(i, i + 1) for i in range(count - 1)]
        backward = [(i + 1, i) for i in range(count - 1)]
        tiles.append(lax.ppermute(tile, axis, forward))
        tiles.append(lax.ppermute(tile, axis, backward))
    return jnp.stack(tiles)


def normalize(values):
    center = values - jnp.mean(values, axis=-1, keepdims=True)
    inverse = lax.rsqrt(jnp.mean(center * center, axis=-1, keepdims=True) + eps)
    return (center * inverse, inverse)


def silu_slope(values):
    logistic = jax.nn.sigmoid(values)
    return logistic * (1.0 + values * (1.0 - logistic))


def transposed_times(operand, second, precision=None):
    return lax.dot_general(
        operand,
        second,
        (((0,), (0,)), ((), ())),
        precision=precision,
        preferred_element_type=jnp.float32,
    )


def times_transposed(operand, second):
    return lax.dot_general(
        operand, second, (((1,), (1,)), ((), ())), preferred_element_type=jnp.float32
    )


def coarse_forward(pooled, w_coarse):
    coarse_norm, inverse = normalize(pooled)
    coarse = coarse_norm.astype(jnp.bfloat16)
    coarse_pre = jnp.dot(coarse, w_coarse, preferred_element_type=jnp.float32)
    return (coarse_norm, inverse, coarse, coarse_pre, jax.nn.silu(coarse_pre).astype(jnp.bfloat16))


def coarse_backward(coarse_cot, coarse_norm, inverse, coarse_pre, w_coarse):
    coarse_delta = (coarse_cot * silu_slope(coarse_pre)).astype(jnp.bfloat16)
    coarse_back = times_transposed(coarse_delta, w_coarse)
    mean_one = jnp.mean(coarse_back, axis=-1, keepdims=True)
    mean_two = jnp.mean(coarse_back * coarse_norm, axis=-1, keepdims=True)
    return (coarse_delta, inverse * (coarse_back - mean_one - coarse_norm * mean_two))


def local(
    features,
    adj_tiles,
    adj_index,
    adj_count,
    bnd_index,
    pool_index,
    w_msg,
    w_update,
    w_coarse,
    cotangent,
):
    feature_count = features.shape[1]
    blocks = adj_tiles.shape[0]
    slot_count = adj_tiles.shape[1]
    tile_rows = adj_tiles.shape[2]
    inputs = features.astype(jnp.float32)
    normed, _ = normalize(inputs)
    scaled = normed.astype(jnp.bfloat16)
    rim_rows = scaled[bnd_index]
    halo_tiles = neighbour_tiles(rim_rows)
    sources = jnp.concatenate(
        [scaled.reshape(blocks, tile_rows, feature_count), halo_tiles], axis=0
    )
    messages = jnp.dot(
        sources.reshape(-1, feature_count), w_msg, preferred_element_type=jnp.float32
    )
    messages = messages.astype(jnp.bfloat16).reshape(sources.shape)
    live_slots = jnp.arange(slot_count)[None, :] < adj_count[:, None]
    masked_tiles = jnp.where(live_slots[:, :, None, None], adj_tiles, jnp.zeros((), jnp.bfloat16))
    aggregated = jnp.einsum(
        "bkij,bkjh->bih", masked_tiles, messages[adj_index], preferred_element_type=jnp.float32
    )
    aggregated = aggregated.astype(jnp.bfloat16).reshape(-1, feature_count)
    summed_scaled = jnp.einsum(
        "bkij,bkjh->bih", masked_tiles, sources[adj_index], preferred_element_type=jnp.float32
    )
    summed_scaled = summed_scaled.astype(jnp.bfloat16).reshape(-1, feature_count)
    w_first = w_update[:feature_count]
    w_second = w_update[feature_count:]
    update_pre = jnp.dot(scaled, w_first, preferred_element_type=jnp.float32) + jnp.dot(
        aggregated, w_second, preferred_element_type=jnp.float32
    )
    hidden_one = inputs + jax.nn.silu(update_pre)
    coarse_count = NC_DEV * lax.axis_size("across")
    assign_float = (pool_index[:, None] == jnp.arange(coarse_count)[None, :]).astype(jnp.float32)
    assign_bits = assign_float.astype(jnp.bfloat16)
    pooled_part = transposed_times(assign_float, hidden_one, lax.Precision.HIGHEST)
    cot_part = transposed_times(assign_bits, cotangent)
    pooled, coarse_cot = all_sum(jnp.stack([pooled_part, cot_part]), "across")
    coarse_norm, inverse, coarse, coarse_pre, coarse_out = coarse_forward(pooled, w_coarse)
    hidden_two = hidden_one + jnp.dot(assign_bits, coarse_out, preferred_element_type=jnp.float32)
    coarse_delta, pooled_delta = coarse_backward(
        coarse_cot, coarse_norm, inverse, coarse_pre, w_coarse
    )
    along_count = lax.axis_size("along")
    across_count = lax.axis_size("across")
    chunk = (feature_count * feature_count) // (along_count * across_count // 2)
    halves = feature_count // chunk
    rows_per_step = across_count // halves
    member = lax.axis_index("across")
    picked_rows = lax.dynamic_index_in_dim(
        coarse.reshape(coarse_count, -1, rows_per_step), member // halves, 2, keepdims=False
    )
    picked_cols = lax.dynamic_index_in_dim(
        coarse_delta.reshape(coarse_count, halves, chunk), member % halves, 1, keepdims=False
    )
    coarse_grad = transposed_times(picked_rows, picked_cols)
    hidden_delta = cotangent.astype(jnp.float32) + jnp.dot(
        assign_float,
        pooled_delta,
        precision=lax.Precision.HIGHEST,
        preferred_element_type=jnp.float32,
    )
    update_delta = (hidden_delta * silu_slope(update_pre)).astype(jnp.bfloat16)
    aggregated_delta = times_transposed(update_delta, w_second).astype(jnp.bfloat16)
    message_grad = transposed_times(summed_scaled, aggregated_delta)
    message_pieces = message_grad.reshape(-1, across_count, chunk).transpose(1, 0, 2)
    message_part = scatter_sum(message_pieces, "across")
    grad_pieces = jnp.concatenate([message_part, coarse_grad], axis=0)
    weight_grads = scatter_sum(grad_pieces, "along")
    return (hidden_two.astype(jnp.bfloat16), weight_grads)


def solution(mesh):
    return jax.shard_map(
        local,
        mesh=mesh,
        in_specs=(
            P(("along", "across"), None),
            P(("along", "across"), None, None, None),
            P(("along", "across"), None),
            P(("along", "across")),
            P(("along", "across")),
            P(("along", "across")),
            P(),
            P(),
            P(),
            P(("along", "across"), None),
        ),
        out_specs=(P(("along", "across"), None), P(("along", "across"))),
        check_vma=False,
    )
```

```python
import jax
import jax.numpy as jnp
from jax import lax
from jax.sharding import PartitionSpec as P

NC_DEV = 4


eps = 1e-05


def scatter_sum(pieces, axes, dim=0):
    return lax.all_to_all(pieces, axes, dim, dim, tiled=False).sum(dim)


def all_sum(values, axis):
    count = lax.axis_size(axis)
    width = values.shape[-1]
    mine = scatter_sum(values.reshape(count, -1, width), axis)
    gathered = lax.all_to_all(jnp.broadcast_to(mine, (count,) + mine.shape), axis, 0, 0, tiled=False)
    return gathered.reshape(values.shape)


def neighbour_tiles(tile):
    tiles = []
    for axis in ("along", "across"):
        count = lax.axis_size(axis)
        forward = [(i, i + 1) for i in range(count - 1)]
        backward = [(i + 1, i) for i in range(count - 1)]
        tiles.append(lax.ppermute(tile, axis, forward))
        tiles.append(lax.ppermute(tile, axis, backward))
    return jnp.stack(tiles)


def normalize(values):
    center = values - jnp.mean(values, axis=-1, keepdims=True)
    inverse = lax.rsqrt(jnp.mean(center * center, axis=-1, keepdims=True) + eps)
    return (center * inverse, inverse)


def silu_slope(values):
    logistic = jax.nn.sigmoid(values)
    return logistic * (1.0 + values * (1.0 - logistic))


def transposed_times(operand, second, precision=None):
    return lax.dot_general(
        operand,
        second,
        (((0,), (0,)), ((), ())),
        precision=precision,
        preferred_element_type=jnp.float32,
    )


def times_transposed(operand, second):
    return lax.dot_general(
        operand, second, (((1,), (1,)), ((), ())), preferred_element_type=jnp.float32
    )


def coarse_forward(pooled, w_coarse):
    coarse_norm, inverse = normalize(pooled)
    coarse = coarse_norm.astype(jnp.bfloat16)
    coarse_pre = jnp.dot(coarse, w_coarse, preferred_element_type=jnp.float32)
    return (coarse_norm, inverse, coarse, coarse_pre, jax.nn.silu(coarse_pre).astype(jnp.bfloat16))


def coarse_backward(coarse_cot, coarse_norm, inverse, coarse_pre, w_coarse):
    coarse_delta = (coarse_cot * silu_slope(coarse_pre)).astype(jnp.bfloat16)
    coarse_back = times_transposed(coarse_delta, w_coarse)
    mean_one = jnp.mean(coarse_back, axis=-1, keepdims=True)
    mean_two = jnp.mean(coarse_back * coarse_norm, axis=-1, keepdims=True)
    return (coarse_delta, inverse * (coarse_back - mean_one - coarse_norm * mean_two))


def local(
    features,
    adj_tiles,
    adj_index,
    adj_count,
    bnd_index,
    pool_index,
    w_msg,
    w_update,
    w_coarse,
    cotangent,
):
    feature_count = features.shape[1]
    blocks = adj_tiles.shape[0]
    slot_count = adj_tiles.shape[1]
    tile_rows = adj_tiles.shape[2]
    inputs = features.astype(jnp.float32)
    normed, _ = normalize(inputs)
    scaled = normed.astype(jnp.bfloat16)
    rim_rows = scaled[bnd_index]
    halo_tiles = neighbour_tiles(rim_rows)
    sources = jnp.concatenate(
        [scaled.reshape(blocks, tile_rows, feature_count), halo_tiles], axis=0
    )
    messages = jnp.dot(
        sources.reshape(-1, feature_count), w_msg, preferred_element_type=jnp.float32
    )
    messages = messages.astype(jnp.bfloat16).reshape(sources.shape)
    live_slots = jnp.arange(slot_count)[None, :] < adj_count[:, None]
    masked_tiles = jnp.where(live_slots[:, :, None, None], adj_tiles, jnp.zeros((), jnp.bfloat16))
    aggregated = jnp.einsum(
        "bkij,bkjh->bih", masked_tiles, messages[adj_index], preferred_element_type=jnp.float32
    )
    aggregated = aggregated.astype(jnp.bfloat16).reshape(-1, feature_count)
    summed_scaled = jnp.einsum(
        "bkij,bkjh->bih", masked_tiles, sources[adj_index], preferred_element_type=jnp.float32
    )
    summed_scaled = summed_scaled.astype(jnp.bfloat16).reshape(-1, feature_count)
    w_first = w_update[:feature_count]
    w_second = w_update[feature_count:]
    update_pre = jnp.dot(scaled, w_first, preferred_element_type=jnp.float32) + jnp.dot(
        aggregated, w_second, preferred_element_type=jnp.float32
    )
    hidden_one = inputs + jax.nn.silu(update_pre)
    coarse_count = NC_DEV * lax.axis_size("across")
    assign_float = (pool_index[:, None] == jnp.arange(coarse_count)[None, :]).astype(jnp.float32)
    assign_bits = assign_float.astype(jnp.bfloat16)
    pooled_part = transposed_times(assign_float, hidden_one, lax.Precision.HIGHEST)
    cot_part = transposed_times(assign_bits, cotangent)
    pooled, coarse_cot = all_sum(jnp.stack([pooled_part, cot_part]), "across")
    coarse_norm, inverse, coarse, coarse_pre, coarse_out = coarse_forward(pooled, w_coarse)
    hidden_two = hidden_one + jnp.dot(assign_bits, coarse_out, preferred_element_type=jnp.float32)
    coarse_delta, pooled_delta = coarse_backward(
        coarse_cot, coarse_norm, inverse, coarse_pre, w_coarse
    )
    along_count = lax.axis_size("along")
    across_count = lax.axis_size("across")
    chunk = (feature_count * feature_count) // (along_count * across_count // 2)
    halves = feature_count // chunk
    rows_per_step = across_count // halves
    member = lax.axis_index("across")
    picked_rows = lax.dynamic_index_in_dim(
        coarse.reshape(coarse_count, -1, rows_per_step), member // halves, 2, keepdims=False
    )
    picked_cols = lax.dynamic_index_in_dim(
        coarse_delta.reshape(coarse_count, halves, chunk), member % halves, 1, keepdims=False
    )
    coarse_grad = transposed_times(picked_rows, picked_cols)
    hidden_delta = cotangent.astype(jnp.float32) + jnp.dot(
        assign_float,
        pooled_delta,
        precision=lax.Precision.HIGHEST,
        preferred_element_type=jnp.float32,
    )
    update_delta = (hidden_delta * silu_slope(update_pre)).astype(jnp.bfloat16)
    aggregated_delta = times_transposed(update_delta, w_second).astype(jnp.bfloat16)
    message_grad = transposed_times(summed_scaled, aggregated_delta)
    message_part = scatter_sum(message_grad.reshape(-1, across_count, chunk), "across", 1)
    grad_pieces = jnp.concatenate([message_part, coarse_grad], axis=0)
    weight_grads = scatter_sum(grad_pieces, "along")
    return (hidden_two.astype(jnp.bfloat16), weight_grads)


def solution(mesh):
    return jax.shard_map(
        local,
        mesh=mesh,
        in_specs=(
            P(("along", "across"), None),
            P(("along", "across"), None, None, None),
            P(("along", "across"), None),
            P(("along", "across")),
            P(("along", "across")),
            P(("along", "across")),
            P(),
            P(),
            P(),
            P(("along", "across"), None),
        ),
        out_specs=(P(("along", "across"), None), P(("along", "across"))),
        check_vma=False,
    )
```

```python
import jax
import jax.numpy as jnp
from jax import lax
from jax.experimental import pallas as pl
from jax.experimental.pallas import tpu as pltpu
from jax.sharding import PartitionSpec as P

NC_DEV = 4


eps = 1e-05


def scatter_sum(pieces, axes, dim=0):
    return lax.all_to_all(pieces, axes, dim, dim, tiled=False).sum(dim)


def all_sum(values, axis):
    count = lax.axis_size(axis)
    width = values.shape[-1]
    mine = scatter_sum(values.reshape(count, -1, width), axis)
    gathered = lax.all_to_all(jnp.broadcast_to(mine, (count,) + mine.shape), axis, 0, 0, tiled=False)
    return gathered.reshape(values.shape)


def neighbour_tiles(tile):
    tiles = []
    for axis in ("along", "across"):
        count = lax.axis_size(axis)
        forward = [(i, i + 1) for i in range(count - 1)]
        backward = [(i + 1, i) for i in range(count - 1)]
        tiles.append(lax.ppermute(tile, axis, forward))
        tiles.append(lax.ppermute(tile, axis, backward))
    return jnp.stack(tiles)


def aggregate_kernel(index_ref, count_ref, tiles_ref, messages_ref, sources_ref, agg_ref, summed_ref):
    block = pl.program_id(0)
    slots = tiles_ref.shape[1]
    last = messages_ref.shape[0] - 1
    agg = jnp.zeros(agg_ref.shape[1:], jnp.float32)
    summed = jnp.zeros(summed_ref.shape[1:], jnp.float32)
    for slot in range(slots):
        source = jnp.clip(index_ref[block, slot], 0, last)
        tile = tiles_ref[0, slot]
        tile = jnp.where(slot < count_ref[block], tile, jnp.zeros_like(tile))
        agg = agg + jnp.dot(tile, messages_ref[source], preferred_element_type=jnp.float32)
        summed = summed + jnp.dot(tile, sources_ref[source], preferred_element_type=jnp.float32)
    agg_ref[0] = agg.astype(agg_ref.dtype)
    summed_ref[0] = summed.astype(summed_ref.dtype)

def aggregate(adj_tiles, adj_index, adj_count, messages, sources):
    blocks, slots, rows, _ = adj_tiles.shape
    count, _, width = messages.shape
    out = jax.ShapeDtypeStruct((blocks, rows, width), jnp.bfloat16)
    return pl.pallas_call(
        aggregate_kernel,
        grid_spec=pltpu.PrefetchScalarGridSpec(
            num_scalar_prefetch=2,
            grid=(blocks,),
            in_specs=[
                pl.BlockSpec((1, slots, rows, rows), lambda b, i, c: (b, 0, 0, 0)),
                pl.BlockSpec((count, rows, width), lambda b, i, c: (0, 0, 0)),
                pl.BlockSpec((count, rows, width), lambda b, i, c: (0, 0, 0)),
            ],
            out_specs=[
                pl.BlockSpec((1, rows, width), lambda b, i, c: (b, 0, 0)),
                pl.BlockSpec((1, rows, width), lambda b, i, c: (b, 0, 0)),
            ],
        ),
        out_shape=(out, out),
    )(adj_index, adj_count, adj_tiles, messages, sources)

def normalize(values):
    center = values - jnp.mean(values, axis=-1, keepdims=True)
    inverse = lax.rsqrt(jnp.mean(center * center, axis=-1, keepdims=True) + eps)
    return (center * inverse, inverse)


def silu_slope(values):
    logistic = jax.nn.sigmoid(values)
    return logistic * (1.0 + values * (1.0 - logistic))


def transposed_times(operand, second, precision=None):
    return lax.dot_general(
        operand,
        second,
        (((0,), (0,)), ((), ())),
        precision=precision,
        preferred_element_type=jnp.float32,
    )


def times_transposed(operand, second):
    return lax.dot_general(
        operand, second, (((1,), (1,)), ((), ())), preferred_element_type=jnp.float32
    )


def coarse_forward(pooled, w_coarse):
    coarse_norm, inverse = normalize(pooled)
    coarse = coarse_norm.astype(jnp.bfloat16)
    coarse_pre = jnp.dot(coarse, w_coarse, preferred_element_type=jnp.float32)
    return (coarse_norm, inverse, coarse, coarse_pre, jax.nn.silu(coarse_pre).astype(jnp.bfloat16))


def coarse_backward(coarse_cot, coarse_norm, inverse, coarse_pre, w_coarse):
    coarse_delta = (coarse_cot * silu_slope(coarse_pre)).astype(jnp.bfloat16)
    coarse_back = times_transposed(coarse_delta, w_coarse)
    mean_one = jnp.mean(coarse_back, axis=-1, keepdims=True)
    mean_two = jnp.mean(coarse_back * coarse_norm, axis=-1, keepdims=True)
    return (coarse_delta, inverse * (coarse_back - mean_one - coarse_norm * mean_two))


def local(
    features,
    adj_tiles,
    adj_index,
    adj_count,
    bnd_index,
    pool_index,
    w_msg,
    w_update,
    w_coarse,
    cotangent,
):
    feature_count = features.shape[1]
    blocks = adj_tiles.shape[0]
    slot_count = adj_tiles.shape[1]
    tile_rows = adj_tiles.shape[2]
    inputs = features.astype(jnp.float32)
    normed, _ = normalize(inputs)
    scaled = normed.astype(jnp.bfloat16)
    rim_rows = scaled[bnd_index]
    halo_tiles = neighbour_tiles(rim_rows)
    sources = jnp.concatenate(
        [scaled.reshape(blocks, tile_rows, feature_count), halo_tiles], axis=0
    )
    messages = jnp.dot(
        sources.reshape(-1, feature_count), w_msg, preferred_element_type=jnp.float32
    )
    messages = messages.astype(jnp.bfloat16).reshape(sources.shape)
    aggregated, summed_scaled = aggregate(adj_tiles, adj_index, adj_count, messages, sources)
    aggregated = aggregated.reshape(-1, feature_count)
    summed_scaled = summed_scaled.reshape(-1, feature_count)
    w_first = w_update[:feature_count]
    w_second = w_update[feature_count:]
    update_pre = jnp.dot(scaled, w_first, preferred_element_type=jnp.float32) + jnp.dot(
        aggregated, w_second, preferred_element_type=jnp.float32
    )
    hidden_one = inputs + jax.nn.silu(update_pre)
    coarse_count = NC_DEV * lax.axis_size("across")
    assign_float = (pool_index[:, None] == jnp.arange(coarse_count)[None, :]).astype(jnp.float32)
    assign_bits = assign_float.astype(jnp.bfloat16)
    pooled_part = transposed_times(assign_float, hidden_one, lax.Precision.HIGHEST)
    cot_part = transposed_times(assign_bits, cotangent)
    pooled, coarse_cot = all_sum(jnp.stack([pooled_part, cot_part]), "across")
    coarse_norm, inverse, coarse, coarse_pre, coarse_out = coarse_forward(pooled, w_coarse)
    hidden_two = hidden_one + jnp.dot(assign_bits, coarse_out, preferred_element_type=jnp.float32)
    coarse_delta, pooled_delta = coarse_backward(
        coarse_cot, coarse_norm, inverse, coarse_pre, w_coarse
    )
    along_count = lax.axis_size("along")
    across_count = lax.axis_size("across")
    chunk = (feature_count * feature_count) // (along_count * across_count // 2)
    halves = feature_count // chunk
    rows_per_step = across_count // halves
    member = lax.axis_index("across")
    picked_rows = lax.dynamic_index_in_dim(
        coarse.reshape(coarse_count, -1, rows_per_step), member // halves, 2, keepdims=False
    )
    picked_cols = lax.dynamic_index_in_dim(
        coarse_delta.reshape(coarse_count, halves, chunk), member % halves, 1, keepdims=False
    )
    coarse_grad = transposed_times(picked_rows, picked_cols)
    hidden_delta = cotangent.astype(jnp.float32) + jnp.dot(
        assign_float,
        pooled_delta,
        precision=lax.Precision.HIGHEST,
        preferred_element_type=jnp.float32,
    )
    update_delta = (hidden_delta * silu_slope(update_pre)).astype(jnp.bfloat16)
    aggregated_delta = times_transposed(update_delta, w_second).astype(jnp.bfloat16)
    message_grad = transposed_times(summed_scaled, aggregated_delta)
    message_part = scatter_sum(message_grad.reshape(-1, across_count, chunk), "across", 1)
    grad_pieces = jnp.concatenate([message_part, coarse_grad], axis=0)
    weight_grads = scatter_sum(grad_pieces, "along")
    return (hidden_two.astype(jnp.bfloat16), weight_grads)


def solution(mesh):
    return jax.shard_map(
        local,
        mesh=mesh,
        in_specs=(
            P(("along", "across"), None),
            P(("along", "across"), None, None, None),
            P(("along", "across"), None),
            P(("along", "across")),
            P(("along", "across")),
            P(("along", "across")),
            P(),
            P(),
            P(),
            P(("along", "across"), None),
        ),
        out_specs=(P(("along", "across"), None), P(("along", "across"))),
        check_vma=False,
    )
```

```python
import jax
import jax.numpy as jnp
from jax import lax
from jax.sharding import PartitionSpec as P

NC_DEV = 4
ALONG = ("z", "x")
ACROSS = ("y", "core")
CHIP_X = 8
CHIP_CORES = 2


eps = 1e-05


def scatter_sum(pieces, axes, dim=0):
    return lax.all_to_all(pieces, axes, dim, dim, tiled=False).sum(dim)


def all_sum(values, axis):
    count = lax.axis_size(axis)
    width = values.shape[-1]
    mine = scatter_sum(values.reshape(count, -1, width), axis)
    gathered = lax.all_to_all(jnp.broadcast_to(mine, (count,) + mine.shape), axis, 0, 0, tiled=False)
    return gathered.reshape(values.shape)


def neighbour_tiles(tile):
    tiles = []
    for axis in (ALONG, ACROSS):
        count = lax.axis_size(axis)
        forward = [(i, i + 1) for i in range(count - 1)]
        backward = [(i + 1, i) for i in range(count - 1)]
        tiles.append(lax.ppermute(tile, axis, forward))
        tiles.append(lax.ppermute(tile, axis, backward))
    return jnp.stack(tiles)


def normalize(values):
    center = values - jnp.mean(values, axis=-1, keepdims=True)
    inverse = lax.rsqrt(jnp.mean(center * center, axis=-1, keepdims=True) + eps)
    return (center * inverse, inverse)


def silu_slope(values):
    logistic = jax.nn.sigmoid(values)
    return logistic * (1.0 + values * (1.0 - logistic))


def transposed_times(operand, second, precision=None):
    return lax.dot_general(
        operand,
        second,
        (((0,), (0,)), ((), ())),
        precision=precision,
        preferred_element_type=jnp.float32,
    )


def times_transposed(operand, second):
    return lax.dot_general(
        operand, second, (((1,), (1,)), ((), ())), preferred_element_type=jnp.float32
    )


def coarse_forward(pooled, w_coarse):
    coarse_norm, inverse = normalize(pooled)
    coarse = coarse_norm.astype(jnp.bfloat16)
    coarse_pre = jnp.dot(coarse, w_coarse, preferred_element_type=jnp.float32)
    return (coarse_norm, inverse, coarse, coarse_pre, jax.nn.silu(coarse_pre).astype(jnp.bfloat16))


def coarse_backward(coarse_cot, coarse_norm, inverse, coarse_pre, w_coarse):
    coarse_delta = (coarse_cot * silu_slope(coarse_pre)).astype(jnp.bfloat16)
    coarse_back = times_transposed(coarse_delta, w_coarse)
    mean_one = jnp.mean(coarse_back, axis=-1, keepdims=True)
    mean_two = jnp.mean(coarse_back * coarse_norm, axis=-1, keepdims=True)
    return (coarse_delta, inverse * (coarse_back - mean_one - coarse_norm * mean_two))


def local(
    features,
    adj_tiles,
    adj_index,
    adj_count,
    bnd_index,
    pool_index,
    w_msg,
    w_update,
    w_coarse,
    cotangent,
):
    feature_count = features.shape[1]
    blocks = adj_tiles.shape[0]
    slot_count = adj_tiles.shape[1]
    tile_rows = adj_tiles.shape[2]
    inputs = features.astype(jnp.float32)
    normed, _ = normalize(inputs)
    scaled = normed.astype(jnp.bfloat16)
    rim_rows = scaled[bnd_index]
    halo_tiles = neighbour_tiles(rim_rows)
    sources = jnp.concatenate(
        [scaled.reshape(blocks, tile_rows, feature_count), halo_tiles], axis=0
    )
    messages = jnp.dot(
        sources.reshape(-1, feature_count), w_msg, preferred_element_type=jnp.float32
    )
    messages = messages.astype(jnp.bfloat16).reshape(sources.shape)
    live_slots = jnp.arange(slot_count)[None, :] < adj_count[:, None]
    masked_tiles = jnp.where(live_slots[:, :, None, None], adj_tiles, jnp.zeros((), jnp.bfloat16))
    aggregated = jnp.einsum(
        "bkij,bkjh->bih", masked_tiles, messages[adj_index], preferred_element_type=jnp.float32
    )
    aggregated = aggregated.astype(jnp.bfloat16).reshape(-1, feature_count)
    summed_scaled = jnp.einsum(
        "bkij,bkjh->bih", masked_tiles, sources[adj_index], preferred_element_type=jnp.float32
    )
    summed_scaled = summed_scaled.astype(jnp.bfloat16).reshape(-1, feature_count)
    w_first = w_update[:feature_count]
    w_second = w_update[feature_count:]
    update_pre = jnp.dot(scaled, w_first, preferred_element_type=jnp.float32) + jnp.dot(
        aggregated, w_second, preferred_element_type=jnp.float32
    )
    hidden_one = inputs + jax.nn.silu(update_pre)
    coarse_count = NC_DEV * lax.axis_size(ACROSS)
    assign_float = (pool_index[:, None] == jnp.arange(coarse_count)[None, :]).astype(jnp.float32)
    assign_bits = assign_float.astype(jnp.bfloat16)
    pooled_part = transposed_times(assign_float, hidden_one, lax.Precision.HIGHEST)
    cot_part = transposed_times(assign_bits, cotangent)
    pooled, coarse_cot = all_sum(jnp.stack([pooled_part, cot_part]), ACROSS)
    coarse_norm, inverse, coarse, coarse_pre, coarse_out = coarse_forward(pooled, w_coarse)
    hidden_two = hidden_one + jnp.dot(assign_bits, coarse_out, preferred_element_type=jnp.float32)
    coarse_delta, pooled_delta = coarse_backward(
        coarse_cot, coarse_norm, inverse, coarse_pre, w_coarse
    )
    along_count = lax.axis_size(ALONG)
    across_count = lax.axis_size(ACROSS)
    chunk = (feature_count * feature_count) // (along_count * across_count // 2)
    halves = feature_count // chunk
    rows_per_step = across_count // halves
    member = lax.axis_index(ACROSS)
    picked_rows = lax.dynamic_index_in_dim(
        coarse.reshape(coarse_count, -1, rows_per_step), member // halves, 2, keepdims=False
    )
    picked_cols = lax.dynamic_index_in_dim(
        coarse_delta.reshape(coarse_count, halves, chunk), member % halves, 1, keepdims=False
    )
    coarse_grad = transposed_times(picked_rows, picked_cols)
    hidden_delta = cotangent.astype(jnp.float32) + jnp.dot(
        assign_float,
        pooled_delta,
        precision=lax.Precision.HIGHEST,
        preferred_element_type=jnp.float32,
    )
    update_delta = (hidden_delta * silu_slope(update_pre)).astype(jnp.bfloat16)
    aggregated_delta = times_transposed(update_delta, w_second).astype(jnp.bfloat16)
    message_grad = transposed_times(summed_scaled, aggregated_delta)
    message_part = scatter_sum(message_grad.reshape(-1, across_count, chunk), ACROSS, 1)
    grad_pieces = jnp.concatenate([message_part, coarse_grad], axis=0)
    along_pieces = grad_pieces.reshape(-1, lax.axis_size("x"), chunk)
    weight_grads = scatter_sum(scatter_sum(along_pieces, "x", 1), "z")
    return (hidden_two.astype(jnp.bfloat16), weight_grads)


def solution(mesh):
    along, across = mesh.shape["along"], mesh.shape["across"]
    chips = jax.sharding.Mesh(
        mesh.devices.reshape(along // CHIP_X, CHIP_X, across // CHIP_CORES, CHIP_CORES),
        ("z", "x", "y", "core"),
    )
    rows = ALONG + ACROSS
    return jax.shard_map(
        local,
        mesh=chips,
        in_specs=(
            P(rows, None),
            P(rows, None, None, None),
            P(rows, None),
            P(rows),
            P(rows),
            P(rows),
            P(),
            P(),
            P(),
            P(rows, None),
        ),
        out_specs=(P(rows, None), P(rows)),
        check_vma=False,
    )
```

```python
import jax
import jax.numpy as jnp
from jax import lax
from jax.sharding import PartitionSpec as P

NC_DEV = 4


eps = 1e-05


def scatter_sum(pieces, axes, dim=0):
    return lax.all_to_all(pieces, axes, dim, dim, tiled=False).sum(dim)


def all_sum(values, axis):
    count = lax.axis_size(axis)
    width = values.shape[-1]
    mine = scatter_sum(values.reshape(count, -1, width), axis)
    gathered = lax.all_to_all(jnp.broadcast_to(mine, (count,) + mine.shape), axis, 0, 0, tiled=False)
    return gathered.reshape(values.shape)


def neighbour_tiles(tile):
    tiles = []
    for axis in ("along", "across"):
        count = lax.axis_size(axis)
        forward = [(i, i + 1) for i in range(count - 1)]
        backward = [(i + 1, i) for i in range(count - 1)]
        tiles.append(lax.ppermute(tile, axis, forward))
        tiles.append(lax.ppermute(tile, axis, backward))
    return jnp.stack(tiles)


def normalize(values):
    center = values - jnp.mean(values, axis=-1, keepdims=True)
    inverse = lax.rsqrt(jnp.mean(center * center, axis=-1, keepdims=True) + eps)
    return (center * inverse, inverse)


def silu_slope(values):
    logistic = jax.nn.sigmoid(values)
    return logistic * (1.0 + values * (1.0 - logistic))


def transposed_times(operand, second, precision=None):
    return lax.dot_general(
        operand,
        second,
        (((0,), (0,)), ((), ())),
        precision=precision,
        preferred_element_type=jnp.float32,
    )


def times_transposed(operand, second):
    return lax.dot_general(
        operand, second, (((1,), (1,)), ((), ())), preferred_element_type=jnp.float32
    )


def coarse_forward(pooled, w_coarse):
    coarse_norm, inverse = normalize(pooled)
    coarse = coarse_norm.astype(jnp.bfloat16)
    coarse_pre = jnp.dot(coarse, w_coarse, preferred_element_type=jnp.float32)
    return (coarse_norm, inverse, coarse, coarse_pre, jax.nn.silu(coarse_pre).astype(jnp.bfloat16))


def coarse_backward(coarse_cot, coarse_norm, inverse, coarse_pre, w_coarse):
    coarse_delta = (coarse_cot * silu_slope(coarse_pre)).astype(jnp.bfloat16)
    coarse_back = times_transposed(coarse_delta, w_coarse)
    mean_one = jnp.mean(coarse_back, axis=-1, keepdims=True)
    mean_two = jnp.mean(coarse_back * coarse_norm, axis=-1, keepdims=True)
    return (coarse_delta, inverse * (coarse_back - mean_one - coarse_norm * mean_two))


def local(
    features,
    adj_tiles,
    adj_index,
    adj_count,
    bnd_index,
    pool_index,
    w_msg,
    w_update,
    w_coarse,
    cotangent,
):
    feature_count = features.shape[1]
    blocks = adj_tiles.shape[0]
    slot_count = adj_tiles.shape[1]
    tile_rows = adj_tiles.shape[2]
    inputs = features.astype(jnp.float32)
    normed, _ = normalize(inputs)
    scaled = normed.astype(jnp.bfloat16)
    node_count = scaled.shape[0]
    pick = (bnd_index[:, None] == jnp.arange(node_count)[None, :]).astype(jnp.bfloat16)
    rim_rows = jnp.dot(pick, scaled, preferred_element_type=jnp.float32).astype(jnp.bfloat16)
    halo_tiles = neighbour_tiles(rim_rows)
    sources = jnp.concatenate(
        [scaled.reshape(blocks, tile_rows, feature_count), halo_tiles], axis=0
    )
    messages = jnp.dot(
        sources.reshape(-1, feature_count), w_msg, preferred_element_type=jnp.float32
    )
    messages = messages.astype(jnp.bfloat16).reshape(sources.shape)
    live_slots = jnp.arange(slot_count)[None, :] < adj_count[:, None]
    masked_tiles = jnp.where(live_slots[:, :, None, None], adj_tiles, jnp.zeros((), jnp.bfloat16))
    aggregated = jnp.einsum(
        "bkij,bkjh->bih", masked_tiles, messages[adj_index], preferred_element_type=jnp.float32
    )
    aggregated = aggregated.astype(jnp.bfloat16).reshape(-1, feature_count)
    summed_scaled = jnp.einsum(
        "bkij,bkjh->bih", masked_tiles, sources[adj_index], preferred_element_type=jnp.float32
    )
    summed_scaled = summed_scaled.astype(jnp.bfloat16).reshape(-1, feature_count)
    w_first = w_update[:feature_count]
    w_second = w_update[feature_count:]
    update_pre = jnp.dot(scaled, w_first, preferred_element_type=jnp.float32) + jnp.dot(
        aggregated, w_second, preferred_element_type=jnp.float32
    )
    hidden_one = inputs + jax.nn.silu(update_pre)
    coarse_count = NC_DEV * lax.axis_size("across")
    assign_float = (pool_index[:, None] == jnp.arange(coarse_count)[None, :]).astype(jnp.float32)
    assign_bits = assign_float.astype(jnp.bfloat16)
    pooled_part = transposed_times(assign_float, hidden_one, lax.Precision.HIGHEST)
    cot_part = transposed_times(assign_bits, cotangent)
    pooled, coarse_cot = all_sum(jnp.stack([pooled_part, cot_part]), "across")
    coarse_norm, inverse, coarse, coarse_pre, coarse_out = coarse_forward(pooled, w_coarse)
    hidden_two = hidden_one + jnp.dot(assign_bits, coarse_out, preferred_element_type=jnp.float32)
    coarse_delta, pooled_delta = coarse_backward(
        coarse_cot, coarse_norm, inverse, coarse_pre, w_coarse
    )
    along_count = lax.axis_size("along")
    across_count = lax.axis_size("across")
    chunk = (feature_count * feature_count) // (along_count * across_count // 2)
    halves = feature_count // chunk
    rows_per_step = across_count // halves
    member = lax.axis_index("across")
    picked_rows = lax.dynamic_index_in_dim(
        coarse.reshape(coarse_count, -1, rows_per_step), member // halves, 2, keepdims=False
    )
    picked_cols = lax.dynamic_index_in_dim(
        coarse_delta.reshape(coarse_count, halves, chunk), member % halves, 1, keepdims=False
    )
    coarse_grad = transposed_times(picked_rows, picked_cols)
    hidden_delta = cotangent.astype(jnp.float32) + jnp.dot(
        assign_float,
        pooled_delta,
        precision=lax.Precision.HIGHEST,
        preferred_element_type=jnp.float32,
    )
    update_delta = (hidden_delta * silu_slope(update_pre)).astype(jnp.bfloat16)
    aggregated_delta = times_transposed(update_delta, w_second).astype(jnp.bfloat16)
    message_grad = transposed_times(summed_scaled, aggregated_delta)
    message_part = scatter_sum(message_grad.reshape(-1, across_count, chunk), "across", 1)
    grad_pieces = jnp.concatenate([message_part, coarse_grad], axis=0)
    weight_grads = scatter_sum(grad_pieces, "along")
    return (hidden_two.astype(jnp.bfloat16), weight_grads)


def solution(mesh):
    return jax.shard_map(
        local,
        mesh=mesh,
        in_specs=(
            P(("along", "across"), None),
            P(("along", "across"), None, None, None),
            P(("along", "across"), None),
            P(("along", "across")),
            P(("along", "across")),
            P(("along", "across")),
            P(),
            P(),
            P(),
            P(("along", "across"), None),
        ),
        out_specs=(P(("along", "across"), None), P(("along", "across"))),
        check_vma=False,
    )
```

```python
import jax
import jax.numpy as jnp
from jax import lax
from jax.sharding import PartitionSpec as P

NC_DEV = 4


eps = 1e-05


def scatter_sum(pieces, axes, dim=0):
    return lax.all_to_all(pieces, axes, dim, dim, tiled=False).sum(dim)


def all_sum(values, axis):
    count = lax.axis_size(axis)
    width = values.shape[-1]
    mine = scatter_sum(values.reshape(count, -1, width), axis)
    gathered = lax.all_to_all(jnp.broadcast_to(mine, (count,) + mine.shape), axis, 0, 0, tiled=False)
    return gathered.reshape(values.shape)


def neighbour_tiles(tile):
    tiles = []
    for axis in ("along", "across"):
        count = lax.axis_size(axis)
        forward = [(i, i + 1) for i in range(count - 1)]
        backward = [(i + 1, i) for i in range(count - 1)]
        tiles.append(lax.ppermute(tile, axis, forward))
        tiles.append(lax.ppermute(tile, axis, backward))
    return jnp.stack(tiles)


def row_sums(values, precision=None):
    ones = jnp.ones((values.shape[-1], 128), values.dtype)
    return jnp.dot(values, ones, precision=precision, preferred_element_type=jnp.float32)


def normalize_rows(features):
    width = features.shape[-1]
    repeat = width // 128
    mean = row_sums(features) / width
    center = features.astype(jnp.float32) - jnp.tile(mean, (1, repeat))
    variance = row_sums(center * center, lax.Precision.HIGHEST) / width
    inverse = lax.rsqrt(variance + eps)
    return center * jnp.tile(inverse, (1, repeat))


def normalize(values):
    center = values - jnp.mean(values, axis=-1, keepdims=True)
    inverse = lax.rsqrt(jnp.mean(center * center, axis=-1, keepdims=True) + eps)
    return (center * inverse, inverse)


def silu_slope(values):
    logistic = jax.nn.sigmoid(values)
    return logistic * (1.0 + values * (1.0 - logistic))


def transposed_times(operand, second, precision=None):
    return lax.dot_general(
        operand,
        second,
        (((0,), (0,)), ((), ())),
        precision=precision,
        preferred_element_type=jnp.float32,
    )


def times_transposed(operand, second):
    return lax.dot_general(
        operand, second, (((1,), (1,)), ((), ())), preferred_element_type=jnp.float32
    )


def coarse_forward(pooled, w_coarse):
    coarse_norm, inverse = normalize(pooled)
    coarse = coarse_norm.astype(jnp.bfloat16)
    coarse_pre = jnp.dot(coarse, w_coarse, preferred_element_type=jnp.float32)
    return (coarse_norm, inverse, coarse, coarse_pre, jax.nn.silu(coarse_pre).astype(jnp.bfloat16))


def coarse_backward(coarse_cot, coarse_norm, inverse, coarse_pre, w_coarse):
    coarse_delta = (coarse_cot * silu_slope(coarse_pre)).astype(jnp.bfloat16)
    coarse_back = times_transposed(coarse_delta, w_coarse)
    mean_one = jnp.mean(coarse_back, axis=-1, keepdims=True)
    mean_two = jnp.mean(coarse_back * coarse_norm, axis=-1, keepdims=True)
    return (coarse_delta, inverse * (coarse_back - mean_one - coarse_norm * mean_two))


def local(
    features,
    adj_tiles,
    adj_index,
    adj_count,
    bnd_index,
    pool_index,
    w_msg,
    w_update,
    w_coarse,
    cotangent,
):
    feature_count = features.shape[1]
    blocks = adj_tiles.shape[0]
    slot_count = adj_tiles.shape[1]
    tile_rows = adj_tiles.shape[2]
    inputs = features.astype(jnp.float32)
    normed = normalize_rows(features)
    scaled = normed.astype(jnp.bfloat16)
    node_count = scaled.shape[0]
    pick = (bnd_index[:, None] == jnp.arange(node_count)[None, :]).astype(jnp.bfloat16)
    rim_rows = jnp.dot(pick, scaled, preferred_element_type=jnp.float32).astype(jnp.bfloat16)
    halo_tiles = neighbour_tiles(rim_rows)
    sources = jnp.concatenate(
        [scaled.reshape(blocks, tile_rows, feature_count), halo_tiles], axis=0
    )
    messages = jnp.dot(
        sources.reshape(-1, feature_count), w_msg, preferred_element_type=jnp.float32
    )
    messages = messages.astype(jnp.bfloat16).reshape(sources.shape)
    live_slots = jnp.arange(slot_count)[None, :] < adj_count[:, None]
    masked_tiles = jnp.where(live_slots[:, :, None, None], adj_tiles, jnp.zeros((), jnp.bfloat16))
    aggregated = jnp.einsum(
        "bkij,bkjh->bih", masked_tiles, messages[adj_index], preferred_element_type=jnp.float32
    )
    aggregated = aggregated.astype(jnp.bfloat16).reshape(-1, feature_count)
    summed_scaled = jnp.einsum(
        "bkij,bkjh->bih", masked_tiles, sources[adj_index], preferred_element_type=jnp.float32
    )
    summed_scaled = summed_scaled.astype(jnp.bfloat16).reshape(-1, feature_count)
    w_first = w_update[:feature_count]
    w_second = w_update[feature_count:]
    update_pre = jnp.dot(scaled, w_first, preferred_element_type=jnp.float32) + jnp.dot(
        aggregated, w_second, preferred_element_type=jnp.float32
    )
    hidden_one = inputs + jax.nn.silu(update_pre)
    coarse_count = NC_DEV * lax.axis_size("across")
    assign_float = (pool_index[:, None] == jnp.arange(coarse_count)[None, :]).astype(jnp.float32)
    assign_bits = assign_float.astype(jnp.bfloat16)
    pooled_part = transposed_times(assign_float, hidden_one, lax.Precision.HIGHEST)
    cot_part = transposed_times(assign_bits, cotangent)
    pooled, coarse_cot = all_sum(jnp.stack([pooled_part, cot_part]), "across")
    coarse_norm, inverse, coarse, coarse_pre, coarse_out = coarse_forward(pooled, w_coarse)
    hidden_two = hidden_one + jnp.dot(assign_bits, coarse_out, preferred_element_type=jnp.float32)
    coarse_delta, pooled_delta = coarse_backward(
        coarse_cot, coarse_norm, inverse, coarse_pre, w_coarse
    )
    along_count = lax.axis_size("along")
    across_count = lax.axis_size("across")
    chunk = (feature_count * feature_count) // (along_count * across_count // 2)
    halves = feature_count // chunk
    rows_per_step = across_count // halves
    member = lax.axis_index("across")
    picked_rows = lax.dynamic_index_in_dim(
        coarse.reshape(coarse_count, -1, rows_per_step), member // halves, 2, keepdims=False
    )
    picked_cols = lax.dynamic_index_in_dim(
        coarse_delta.reshape(coarse_count, halves, chunk), member % halves, 1, keepdims=False
    )
    coarse_grad = transposed_times(picked_rows, picked_cols)
    hidden_delta = cotangent.astype(jnp.float32) + jnp.dot(
        assign_float,
        pooled_delta,
        precision=lax.Precision.HIGHEST,
        preferred_element_type=jnp.float32,
    )
    update_delta = (hidden_delta * silu_slope(update_pre)).astype(jnp.bfloat16)
    aggregated_delta = times_transposed(update_delta, w_second).astype(jnp.bfloat16)
    message_grad = transposed_times(summed_scaled, aggregated_delta)
    message_part = scatter_sum(message_grad.reshape(-1, across_count, chunk), "across", 1)
    grad_pieces = jnp.concatenate([message_part, coarse_grad], axis=0)
    weight_grads = scatter_sum(grad_pieces, "along")
    return (hidden_two.astype(jnp.bfloat16), weight_grads)


def solution(mesh):
    return jax.shard_map(
        local,
        mesh=mesh,
        in_specs=(
            P(("along", "across"), None),
            P(("along", "across"), None, None, None),
            P(("along", "across"), None),
            P(("along", "across")),
            P(("along", "across")),
            P(("along", "across")),
            P(),
            P(),
            P(),
            P(("along", "across"), None),
        ),
        out_specs=(P(("along", "across"), None), P(("along", "across"))),
        check_vma=False,
    )
```

```python
import jax
import jax.numpy as jnp
from jax import lax
from jax.sharding import PartitionSpec as P

NC_DEV = 4


eps = 1e-05


def scatter_sum(pieces, axes, dim=0):
    return lax.all_to_all(pieces, axes, dim, dim, tiled=False).sum(dim)


def all_sum(values, axis):
    count = lax.axis_size(axis)
    width = values.shape[-1]
    mine = scatter_sum(values.reshape(count, -1, width), axis)
    gathered = lax.all_to_all(jnp.broadcast_to(mine, (count,) + mine.shape), axis, 0, 0, tiled=False)
    return gathered.reshape(values.shape)


def neighbour_tiles(tile):
    tiles = []
    for axis in ("along", "across"):
        count = lax.axis_size(axis)
        forward = [(i, i + 1) for i in range(count - 1)]
        backward = [(i + 1, i) for i in range(count - 1)]
        tiles.append(lax.ppermute(tile, axis, forward))
        tiles.append(lax.ppermute(tile, axis, backward))
    return jnp.stack(tiles)


def row_sums(values, precision=None):
    ones = jnp.ones((values.shape[-1], 128), values.dtype)
    return jnp.dot(values, ones, precision=precision, preferred_element_type=jnp.float32)


def normalize_rows(features):
    width = features.shape[-1]
    repeat = width // 128
    mean = row_sums(features) / width
    center = features.astype(jnp.float32) - jnp.tile(mean, (1, repeat))
    variance = row_sums(center * center, lax.Precision.HIGHEST) / width
    inverse = lax.rsqrt(variance + eps)
    return center * jnp.tile(inverse, (1, repeat))


def normalize(values):
    center = values - jnp.mean(values, axis=-1, keepdims=True)
    inverse = lax.rsqrt(jnp.mean(center * center, axis=-1, keepdims=True) + eps)
    return (center * inverse, inverse)


def silu_slope(values):
    logistic = jax.nn.sigmoid(values)
    return logistic * (1.0 + values * (1.0 - logistic))


def transposed_times(operand, second, precision=None):
    return lax.dot_general(
        operand,
        second,
        (((0,), (0,)), ((), ())),
        precision=precision,
        preferred_element_type=jnp.float32,
    )


def times_transposed(operand, second):
    return lax.dot_general(
        operand, second, (((1,), (1,)), ((), ())), preferred_element_type=jnp.float32
    )


def coarse_forward(pooled, w_coarse):
    coarse_norm, inverse = normalize(pooled)
    coarse = coarse_norm.astype(jnp.bfloat16)
    coarse_pre = jnp.dot(coarse, w_coarse, preferred_element_type=jnp.float32)
    return (coarse_norm, inverse, coarse, coarse_pre, jax.nn.silu(coarse_pre).astype(jnp.bfloat16))


def coarse_backward(coarse_cot, coarse_norm, inverse, coarse_pre, w_coarse):
    coarse_delta = (coarse_cot * silu_slope(coarse_pre)).astype(jnp.bfloat16)
    coarse_back = times_transposed(coarse_delta, w_coarse)
    mean_one = jnp.mean(coarse_back, axis=-1, keepdims=True)
    mean_two = jnp.mean(coarse_back * coarse_norm, axis=-1, keepdims=True)
    return (coarse_delta, inverse * (coarse_back - mean_one - coarse_norm * mean_two))


def local(
    features,
    adj_tiles,
    adj_index,
    adj_count,
    bnd_index,
    pool_index,
    w_msg,
    w_update,
    w_coarse,
    cotangent,
):
    feature_count = features.shape[1]
    blocks = adj_tiles.shape[0]
    slot_count = adj_tiles.shape[1]
    tile_rows = adj_tiles.shape[2]
    inputs = features.astype(jnp.float32)
    normed = normalize_rows(features)
    scaled = normed.astype(jnp.bfloat16)
    node_count = scaled.shape[0]
    pick = (bnd_index[:, None] == jnp.arange(node_count)[None, :]).astype(jnp.bfloat16)
    rim_rows = jnp.dot(pick, scaled, preferred_element_type=jnp.float32).astype(jnp.bfloat16)
    halo_tiles = neighbour_tiles(rim_rows)
    sources = jnp.concatenate(
        [scaled.reshape(blocks, tile_rows, feature_count), halo_tiles], axis=0
    )
    messages = jnp.dot(
        sources.reshape(-1, feature_count), w_msg, preferred_element_type=jnp.float32
    )
    messages = messages.astype(jnp.bfloat16).reshape(sources.shape)
    live_slots = jnp.arange(slot_count)[None, :] < adj_count[:, None]
    masked_tiles = jnp.where(live_slots[:, :, None, None], adj_tiles, jnp.zeros((), jnp.bfloat16))
    aggregated = jnp.einsum(
        "bkij,bkjh->bih", masked_tiles, messages[adj_index], preferred_element_type=jnp.float32
    )
    aggregated = aggregated.astype(jnp.bfloat16).reshape(-1, feature_count)
    summed_scaled = jnp.einsum(
        "bkij,bkjh->bih", masked_tiles, sources[adj_index], preferred_element_type=jnp.float32
    )
    summed_scaled = summed_scaled.astype(jnp.bfloat16).reshape(-1, feature_count)
    w_first = w_update[:feature_count]
    w_second = w_update[feature_count:]
    update_pre = jnp.dot(scaled, w_first, preferred_element_type=jnp.float32) + jnp.dot(
        aggregated, w_second, preferred_element_type=jnp.float32
    )
    hidden_one = inputs + jax.nn.silu(update_pre)
    coarse_count = NC_DEV * lax.axis_size("across")
    assign_float = (pool_index[:, None] == jnp.arange(coarse_count)[None, :]).astype(jnp.float32)
    assign_bits = assign_float.astype(jnp.bfloat16)
    pooled_part = transposed_times(assign_float, hidden_one, lax.Precision.HIGHEST)
    cot_part = transposed_times(assign_bits, cotangent)
    pooled, coarse_cot = all_sum(jnp.stack([pooled_part, cot_part]), "across")
    coarse_norm, inverse, coarse, coarse_pre, coarse_out = coarse_forward(pooled, w_coarse)
    hidden_two = hidden_one + jnp.dot(assign_bits, coarse_out, preferred_element_type=jnp.float32)
    coarse_delta, pooled_delta = coarse_backward(
        coarse_cot, coarse_norm, inverse, coarse_pre, w_coarse
    )
    along_count = lax.axis_size("along")
    across_count = lax.axis_size("across")
    chunk = (feature_count * feature_count) // (along_count * across_count // 2)
    halves = feature_count // chunk
    rows_per_step = across_count // halves
    member = lax.axis_index("across")
    picked_cols = lax.dynamic_slice_in_dim(coarse_delta, (member % halves) * chunk, chunk, 1)
    coarse_rows = transposed_times(coarse, picked_cols).reshape(-1, rows_per_step, chunk)
    coarse_grad = lax.dynamic_index_in_dim(coarse_rows, member // halves, 1, keepdims=False)
    hidden_delta = cotangent.astype(jnp.float32) + jnp.dot(
        assign_float,
        pooled_delta,
        precision=lax.Precision.HIGHEST,
        preferred_element_type=jnp.float32,
    )
    update_delta = (hidden_delta * silu_slope(update_pre)).astype(jnp.bfloat16)
    aggregated_delta = times_transposed(update_delta, w_second).astype(jnp.bfloat16)
    message_grad = transposed_times(summed_scaled, aggregated_delta)
    message_part = scatter_sum(message_grad.reshape(-1, across_count, chunk), "across", 1)
    grad_pieces = jnp.concatenate([message_part, coarse_grad], axis=0)
    weight_grads = scatter_sum(grad_pieces, "along")
    return (hidden_two.astype(jnp.bfloat16), weight_grads)


def solution(mesh):
    return jax.shard_map(
        local,
        mesh=mesh,
        in_specs=(
            P(("along", "across"), None),
            P(("along", "across"), None, None, None),
            P(("along", "across"), None),
            P(("along", "across")),
            P(("along", "across")),
            P(("along", "across")),
            P(),
            P(),
            P(),
            P(("along", "across"), None),
        ),
        out_specs=(P(("along", "across"), None), P(("along", "across"))),
        check_vma=False,
    )
```

```python
import jax
import jax.numpy as jnp
from jax import lax
from jax.sharding import PartitionSpec as P

NC_DEV = 4


eps = 1e-05


def scatter_sum(pieces, axes, dim=0):
    return lax.all_to_all(pieces, axes, dim, dim, tiled=False).sum(dim)


def all_sum(values, axis):
    count = lax.axis_size(axis)
    width = values.shape[-1]
    mine = scatter_sum(values.reshape(count, -1, width), axis)
    gathered = lax.all_to_all(jnp.broadcast_to(mine, (count,) + mine.shape), axis, 0, 0, tiled=False)
    return gathered.reshape(values.shape)


def neighbour_tiles(tile):
    tiles = []
    for axis in ("along", "across"):
        count = lax.axis_size(axis)
        forward = [(i, i + 1) for i in range(count - 1)]
        backward = [(i + 1, i) for i in range(count - 1)]
        tiles.append(lax.ppermute(tile, axis, forward))
        tiles.append(lax.ppermute(tile, axis, backward))
    return jnp.stack(tiles)


def row_sums(values, precision=None):
    ones = jnp.ones((values.shape[-1], 128), values.dtype)
    return jnp.dot(values, ones, precision=precision, preferred_element_type=jnp.float32)


def normalize_rows(features):
    width = features.shape[-1]
    repeat = width // 128
    mean = row_sums(features) / width
    center = features.astype(jnp.float32) - jnp.tile(mean, (1, repeat))
    variance = row_sums(center * center, lax.Precision.HIGHEST) / width
    inverse = lax.rsqrt(variance + eps)
    return center * jnp.tile(inverse, (1, repeat))


def normalize(values):
    center = values - jnp.mean(values, axis=-1, keepdims=True)
    inverse = lax.rsqrt(jnp.mean(center * center, axis=-1, keepdims=True) + eps)
    return (center * inverse, inverse)


def silu_slope(values):
    logistic = jax.nn.sigmoid(values)
    return logistic * (1.0 + values * (1.0 - logistic))


def transposed_times(operand, second, precision=None):
    return lax.dot_general(
        operand,
        second,
        (((0,), (0,)), ((), ())),
        precision=precision,
        preferred_element_type=jnp.float32,
    )


def times_transposed(operand, second):
    return lax.dot_general(
        operand, second, (((1,), (1,)), ((), ())), preferred_element_type=jnp.float32
    )


def coarse_forward(pooled, w_coarse):
    coarse_norm, inverse = normalize(pooled)
    coarse = coarse_norm.astype(jnp.bfloat16)
    coarse_pre = jnp.dot(coarse, w_coarse, preferred_element_type=jnp.float32)
    return (coarse_norm, inverse, coarse, coarse_pre, jax.nn.silu(coarse_pre).astype(jnp.bfloat16))


def coarse_backward(coarse_cot, coarse_norm, inverse, coarse_pre, w_coarse):
    coarse_delta = (coarse_cot * silu_slope(coarse_pre)).astype(jnp.bfloat16)
    coarse_back = times_transposed(coarse_delta, w_coarse)
    mean_one = jnp.mean(coarse_back, axis=-1, keepdims=True)
    mean_two = jnp.mean(coarse_back * coarse_norm, axis=-1, keepdims=True)
    return (coarse_delta, inverse * (coarse_back - mean_one - coarse_norm * mean_two))


def local(
    features,
    adj_tiles,
    adj_index,
    adj_count,
    bnd_index,
    pool_index,
    w_msg,
    w_update,
    w_coarse,
    cotangent,
):
    feature_count = features.shape[1]
    blocks = adj_tiles.shape[0]
    slot_count = adj_tiles.shape[1]
    tile_rows = adj_tiles.shape[2]
    inputs = features.astype(jnp.float32)
    normed = normalize_rows(features)
    scaled = normed.astype(jnp.bfloat16)
    node_count = scaled.shape[0]
    pick = (bnd_index[:, None] == jnp.arange(node_count)[None, :]).astype(jnp.bfloat16)
    rim_rows = jnp.dot(pick, scaled, preferred_element_type=jnp.float32).astype(jnp.bfloat16)
    halo_tiles = neighbour_tiles(rim_rows)
    sources = jnp.concatenate(
        [scaled.reshape(blocks, tile_rows, feature_count), halo_tiles], axis=0
    )
    live_slots = jnp.arange(slot_count)[None, :] < adj_count[:, None]
    masked_tiles = jnp.where(live_slots[:, :, None, None], adj_tiles, jnp.zeros((), jnp.bfloat16))
    summed = jnp.einsum(
        "bkij,bkjh->bih", masked_tiles, sources[adj_index], preferred_element_type=jnp.float32
    ).reshape(-1, feature_count)
    summed_high = lax.reduce_precision(summed, exponent_bits=8, mantissa_bits=7)
    summed_scaled = summed_high.astype(jnp.bfloat16)
    summed_low = (summed - summed_high).astype(jnp.bfloat16)
    aggregated = (
        jnp.dot(summed_scaled, w_msg, preferred_element_type=jnp.float32)
        + jnp.dot(summed_low, w_msg, preferred_element_type=jnp.float32)
    ).astype(jnp.bfloat16)
    w_first = w_update[:feature_count]
    w_second = w_update[feature_count:]
    update_pre = jnp.dot(scaled, w_first, preferred_element_type=jnp.float32) + jnp.dot(
        aggregated, w_second, preferred_element_type=jnp.float32
    )
    hidden_one = inputs + jax.nn.silu(update_pre)
    coarse_count = NC_DEV * lax.axis_size("across")
    assign_float = (pool_index[:, None] == jnp.arange(coarse_count)[None, :]).astype(jnp.float32)
    assign_bits = assign_float.astype(jnp.bfloat16)
    pooled_part = transposed_times(assign_float, hidden_one, lax.Precision.HIGHEST)
    cot_part = transposed_times(assign_bits, cotangent)
    pooled, coarse_cot = all_sum(jnp.stack([pooled_part, cot_part]), "across")
    coarse_norm, inverse, coarse, coarse_pre, coarse_out = coarse_forward(pooled, w_coarse)
    hidden_two = hidden_one + jnp.dot(assign_bits, coarse_out, preferred_element_type=jnp.float32)
    coarse_delta, pooled_delta = coarse_backward(
        coarse_cot, coarse_norm, inverse, coarse_pre, w_coarse
    )
    along_count = lax.axis_size("along")
    across_count = lax.axis_size("across")
    chunk = (feature_count * feature_count) // (along_count * across_count // 2)
    halves = feature_count // chunk
    rows_per_step = across_count // halves
    member = lax.axis_index("across")
    picked_cols = lax.dynamic_slice_in_dim(coarse_delta, (member % halves) * chunk, chunk, 1)
    coarse_rows = transposed_times(coarse, picked_cols).reshape(-1, rows_per_step, chunk)
    coarse_grad = lax.dynamic_index_in_dim(coarse_rows, member // halves, 1, keepdims=False)
    hidden_delta = cotangent.astype(jnp.float32) + jnp.dot(
        assign_float,
        pooled_delta,
        precision=lax.Precision.HIGHEST,
        preferred_element_type=jnp.float32,
    )
    update_delta = (hidden_delta * silu_slope(update_pre)).astype(jnp.bfloat16)
    aggregated_delta = times_transposed(update_delta, w_second).astype(jnp.bfloat16)
    message_grad = transposed_times(summed_scaled, aggregated_delta)
    message_part = scatter_sum(message_grad.reshape(-1, across_count, chunk), "across", 1)
    grad_pieces = jnp.concatenate([message_part, coarse_grad], axis=0)
    weight_grads = scatter_sum(grad_pieces, "along")
    return (hidden_two.astype(jnp.bfloat16), weight_grads)


def solution(mesh):
    return jax.shard_map(
        local,
        mesh=mesh,
        in_specs=(
            P(("along", "across"), None),
            P(("along", "across"), None, None, None),
            P(("along", "across"), None),
            P(("along", "across")),
            P(("along", "across")),
            P(("along", "across")),
            P(),
            P(),
            P(),
            P(("along", "across"), None),
        ),
        out_specs=(P(("along", "across"), None), P(("along", "across"))),
        check_vma=False,
    )
```

```python
import jax
import jax.numpy as jnp
from jax import lax
from jax.sharding import PartitionSpec as P

NC_DEV = 4


eps = 1e-05


def scatter_sum(pieces, axes, dim=0):
    return lax.all_to_all(pieces, axes, dim, dim, tiled=False).sum(dim)


def all_sum(values, axis):
    count = lax.axis_size(axis)
    width = values.shape[-1]
    mine = scatter_sum(values.reshape(count, -1, width), axis)
    gathered = lax.all_to_all(jnp.broadcast_to(mine, (count,) + mine.shape), axis, 0, 0, tiled=False)
    return gathered.reshape(values.shape)


def neighbour_tiles(tile):
    tiles = []
    for axis in ("along", "across"):
        count = lax.axis_size(axis)
        forward = [(i, i + 1) for i in range(count - 1)]
        backward = [(i + 1, i) for i in range(count - 1)]
        tiles.append(lax.ppermute(tile, axis, forward))
        tiles.append(lax.ppermute(tile, axis, backward))
    return jnp.stack(tiles)


def row_sums(values, precision=None):
    ones = jnp.ones((values.shape[-1], 128), values.dtype)
    return jnp.dot(values, ones, precision=precision, preferred_element_type=jnp.float32)


def normalize_rows(features):
    width = features.shape[-1]
    repeat = width // 128
    mean = row_sums(features) / width
    center = features.astype(jnp.float32) - jnp.tile(mean, (1, repeat))
    variance = row_sums(center * center, lax.Precision.HIGH) / width
    inverse = lax.rsqrt(variance + eps)
    return center * jnp.tile(inverse, (1, repeat))


def normalize(values):
    center = values - jnp.mean(values, axis=-1, keepdims=True)
    inverse = lax.rsqrt(jnp.mean(center * center, axis=-1, keepdims=True) + eps)
    return (center * inverse, inverse)


def silu_slope(values):
    logistic = jax.nn.sigmoid(values)
    return logistic * (1.0 + values * (1.0 - logistic))


def transposed_times(operand, second, precision=None):
    return lax.dot_general(
        operand,
        second,
        (((0,), (0,)), ((), ())),
        precision=precision,
        preferred_element_type=jnp.float32,
    )


def times_transposed(operand, second):
    return lax.dot_general(
        operand, second, (((1,), (1,)), ((), ())), preferred_element_type=jnp.float32
    )


def coarse_forward(pooled, w_coarse):
    coarse_norm, inverse = normalize(pooled)
    coarse = coarse_norm.astype(jnp.bfloat16)
    coarse_pre = jnp.dot(coarse, w_coarse, preferred_element_type=jnp.float32)
    return (coarse_norm, inverse, coarse, coarse_pre, jax.nn.silu(coarse_pre).astype(jnp.bfloat16))


def coarse_backward(coarse_cot, coarse_norm, inverse, coarse_pre, w_coarse):
    coarse_delta = (coarse_cot * silu_slope(coarse_pre)).astype(jnp.bfloat16)
    coarse_back = times_transposed(coarse_delta, w_coarse)
    mean_one = jnp.mean(coarse_back, axis=-1, keepdims=True)
    mean_two = jnp.mean(coarse_back * coarse_norm, axis=-1, keepdims=True)
    return (coarse_delta, inverse * (coarse_back - mean_one - coarse_norm * mean_two))


def local(
    features,
    adj_tiles,
    adj_index,
    adj_count,
    bnd_index,
    pool_index,
    w_msg,
    w_update,
    w_coarse,
    cotangent,
):
    feature_count = features.shape[1]
    blocks = adj_tiles.shape[0]
    slot_count = adj_tiles.shape[1]
    tile_rows = adj_tiles.shape[2]
    inputs = features.astype(jnp.float32)
    normed = normalize_rows(features)
    scaled = normed.astype(jnp.bfloat16)
    node_count = scaled.shape[0]
    pick = (bnd_index[:, None] == jnp.arange(node_count)[None, :]).astype(jnp.bfloat16)
    rim_rows = jnp.dot(pick, scaled, preferred_element_type=jnp.float32).astype(jnp.bfloat16)
    halo_tiles = neighbour_tiles(rim_rows)
    sources = jnp.concatenate(
        [scaled.reshape(blocks, tile_rows, feature_count), halo_tiles], axis=0
    )
    live_slots = jnp.arange(slot_count)[None, :] < adj_count[:, None]
    masked_tiles = jnp.where(live_slots[:, :, None, None], adj_tiles, jnp.zeros((), jnp.bfloat16))
    summed = jnp.einsum(
        "bkij,bkjh->bih", masked_tiles, sources[adj_index], preferred_element_type=jnp.float32
    ).reshape(-1, feature_count)
    summed_high = lax.reduce_precision(summed, exponent_bits=8, mantissa_bits=7)
    summed_scaled = summed_high.astype(jnp.bfloat16)
    summed_low = (summed - summed_high).astype(jnp.bfloat16)
    aggregated = (
        jnp.dot(summed_scaled, w_msg, preferred_element_type=jnp.float32)
        + jnp.dot(summed_low, w_msg, preferred_element_type=jnp.float32)
    ).astype(jnp.bfloat16)
    w_first = w_update[:feature_count]
    w_second = w_update[feature_count:]
    update_pre = jnp.dot(scaled, w_first, preferred_element_type=jnp.float32) + jnp.dot(
        aggregated, w_second, preferred_element_type=jnp.float32
    )
    hidden_one = inputs + jax.nn.silu(update_pre)
    coarse_count = NC_DEV * lax.axis_size("across")
    assign_float = (pool_index[:, None] == jnp.arange(coarse_count)[None, :]).astype(jnp.float32)
    assign_bits = assign_float.astype(jnp.bfloat16)
    pooled_part = transposed_times(assign_float, hidden_one, lax.Precision.HIGH)
    cot_part = transposed_times(assign_bits, cotangent)
    pooled, coarse_cot = all_sum(jnp.stack([pooled_part, cot_part]), "across")
    coarse_norm, inverse, coarse, coarse_pre, coarse_out = coarse_forward(pooled, w_coarse)
    hidden_two = hidden_one + jnp.dot(assign_bits, coarse_out, preferred_element_type=jnp.float32)
    coarse_delta, pooled_delta = coarse_backward(
        coarse_cot, coarse_norm, inverse, coarse_pre, w_coarse
    )
    along_count = lax.axis_size("along")
    across_count = lax.axis_size("across")
    chunk = (feature_count * feature_count) // (along_count * across_count // 2)
    halves = feature_count // chunk
    rows_per_step = across_count // halves
    member = lax.axis_index("across")
    picked_cols = lax.dynamic_slice_in_dim(coarse_delta, (member % halves) * chunk, chunk, 1)
    coarse_rows = transposed_times(coarse, picked_cols).reshape(-1, rows_per_step, chunk)
    coarse_grad = lax.dynamic_index_in_dim(coarse_rows, member // halves, 1, keepdims=False)
    hidden_delta = cotangent.astype(jnp.float32) + jnp.dot(
        assign_float,
        pooled_delta,
        precision=lax.Precision.HIGH,
        preferred_element_type=jnp.float32,
    )
    update_delta = (hidden_delta * silu_slope(update_pre)).astype(jnp.bfloat16)
    aggregated_delta = times_transposed(update_delta, w_second).astype(jnp.bfloat16)
    message_grad = transposed_times(summed_scaled, aggregated_delta)
    message_part = scatter_sum(message_grad.reshape(-1, across_count, chunk), "across", 1)
    grad_pieces = jnp.concatenate([message_part, coarse_grad], axis=0)
    weight_grads = scatter_sum(grad_pieces, "along")
    return (hidden_two.astype(jnp.bfloat16), weight_grads)


def solution(mesh):
    return jax.shard_map(
        local,
        mesh=mesh,
        in_specs=(
            P(("along", "across"), None),
            P(("along", "across"), None, None, None),
            P(("along", "across"), None),
            P(("along", "across")),
            P(("along", "across")),
            P(("along", "across")),
            P(),
            P(),
            P(),
            P(("along", "across"), None),
        ),
        out_specs=(P(("along", "across"), None), P(("along", "across"))),
        check_vma=False,
    )
```

```python
import jax
import jax.numpy as jnp
from jax import lax
from jax.sharding import PartitionSpec as P

NC_DEV = 4


eps = 1e-05


def scatter_sum(pieces, axes, dim=0):
    return lax.all_to_all(pieces, axes, dim, dim, tiled=False).sum(dim)


def all_sum(values, axis):
    count = lax.axis_size(axis)
    width = values.shape[-1]
    mine = scatter_sum(values.reshape(count, -1, width), axis)
    gathered = lax.all_to_all(jnp.broadcast_to(mine, (count,) + mine.shape), axis, 0, 0, tiled=False)
    return gathered.reshape(values.shape)


def neighbour_tiles(tile):
    tiles = []
    for axis in ("along", "across"):
        count = lax.axis_size(axis)
        forward = [(i, i + 1) for i in range(count - 1)]
        backward = [(i + 1, i) for i in range(count - 1)]
        tiles.append(lax.ppermute(tile, axis, forward))
        tiles.append(lax.ppermute(tile, axis, backward))
    return jnp.stack(tiles)


def row_sums(values, precision=None):
    ones = jnp.ones((values.shape[-1], values.shape[-1]), values.dtype)
    return jnp.dot(values, ones, precision=precision, preferred_element_type=jnp.float32)


def normalize_rows(features):
    width = features.shape[-1]
    mean = row_sums(features) / width
    center = features.astype(jnp.float32) - mean
    variance = row_sums(center * center, lax.Precision.HIGH) / width
    return center * lax.rsqrt(variance + eps)


def normalize(values):
    center = values - jnp.mean(values, axis=-1, keepdims=True)
    inverse = lax.rsqrt(jnp.mean(center * center, axis=-1, keepdims=True) + eps)
    return (center * inverse, inverse)


def silu_slope(values):
    logistic = jax.nn.sigmoid(values)
    return logistic * (1.0 + values * (1.0 - logistic))


def transposed_times(operand, second, precision=None):
    return lax.dot_general(
        operand,
        second,
        (((0,), (0,)), ((), ())),
        precision=precision,
        preferred_element_type=jnp.float32,
    )


def times_transposed(operand, second):
    return lax.dot_general(
        operand, second, (((1,), (1,)), ((), ())), preferred_element_type=jnp.float32
    )


def coarse_forward(pooled, w_coarse):
    coarse_norm, inverse = normalize(pooled)
    coarse = coarse_norm.astype(jnp.bfloat16)
    coarse_pre = jnp.dot(coarse, w_coarse, preferred_element_type=jnp.float32)
    return (coarse_norm, inverse, coarse, coarse_pre, jax.nn.silu(coarse_pre).astype(jnp.bfloat16))


def coarse_backward(coarse_cot, coarse_norm, inverse, coarse_pre, w_coarse):
    coarse_delta = (coarse_cot * silu_slope(coarse_pre)).astype(jnp.bfloat16)
    coarse_back = times_transposed(coarse_delta, w_coarse)
    mean_one = jnp.mean(coarse_back, axis=-1, keepdims=True)
    mean_two = jnp.mean(coarse_back * coarse_norm, axis=-1, keepdims=True)
    return (coarse_delta, inverse * (coarse_back - mean_one - coarse_norm * mean_two))


def local(
    features,
    adj_tiles,
    adj_index,
    adj_count,
    bnd_index,
    pool_index,
    w_msg,
    w_update,
    w_coarse,
    cotangent,
):
    feature_count = features.shape[1]
    blocks = adj_tiles.shape[0]
    slot_count = adj_tiles.shape[1]
    tile_rows = adj_tiles.shape[2]
    inputs = features.astype(jnp.float32)
    normed = normalize_rows(features)
    scaled = normed.astype(jnp.bfloat16)
    node_count = scaled.shape[0]
    pick = (bnd_index[:, None] == jnp.arange(node_count)[None, :]).astype(jnp.bfloat16)
    rim_rows = jnp.dot(pick, scaled, preferred_element_type=jnp.float32).astype(jnp.bfloat16)
    halo_tiles = neighbour_tiles(rim_rows)
    sources = jnp.concatenate(
        [scaled.reshape(blocks, tile_rows, feature_count), halo_tiles], axis=0
    )
    live_slots = jnp.arange(slot_count)[None, :] < adj_count[:, None]
    masked_tiles = jnp.where(live_slots[:, :, None, None], adj_tiles, jnp.zeros((), jnp.bfloat16))
    summed = jnp.einsum(
        "bkij,bkjh->bih", masked_tiles, sources[adj_index], preferred_element_type=jnp.float32
    ).reshape(-1, feature_count)
    summed_high = lax.reduce_precision(summed, exponent_bits=8, mantissa_bits=7)
    summed_scaled = summed_high.astype(jnp.bfloat16)
    summed_low = (summed - summed_high).astype(jnp.bfloat16)
    aggregated = (
        jnp.dot(summed_scaled, w_msg, preferred_element_type=jnp.float32)
        + jnp.dot(summed_low, w_msg, preferred_element_type=jnp.float32)
    ).astype(jnp.bfloat16)
    w_first = w_update[:feature_count]
    w_second = w_update[feature_count:]
    update_pre = jnp.dot(scaled, w_first, preferred_element_type=jnp.float32) + jnp.dot(
        aggregated, w_second, preferred_element_type=jnp.float32
    )
    hidden_one = inputs + jax.nn.silu(update_pre)
    coarse_count = NC_DEV * lax.axis_size("across")
    assign_float = (pool_index[:, None] == jnp.arange(coarse_count)[None, :]).astype(jnp.float32)
    assign_bits = assign_float.astype(jnp.bfloat16)
    pooled_part = transposed_times(assign_float, hidden_one, lax.Precision.HIGH)
    cot_part = transposed_times(assign_bits, cotangent)
    pooled, coarse_cot = all_sum(jnp.stack([pooled_part, cot_part]), "across")
    coarse_norm, inverse, coarse, coarse_pre, coarse_out = coarse_forward(pooled, w_coarse)
    hidden_two = hidden_one + jnp.dot(assign_bits, coarse_out, preferred_element_type=jnp.float32)
    coarse_delta, pooled_delta = coarse_backward(
        coarse_cot, coarse_norm, inverse, coarse_pre, w_coarse
    )
    along_count = lax.axis_size("along")
    across_count = lax.axis_size("across")
    chunk = (feature_count * feature_count) // (along_count * across_count // 2)
    halves = feature_count // chunk
    rows_per_step = across_count // halves
    member = lax.axis_index("across")
    picked_cols = lax.dynamic_slice_in_dim(coarse_delta, (member % halves) * chunk, chunk, 1)
    coarse_rows = transposed_times(coarse, picked_cols).reshape(-1, rows_per_step, chunk)
    coarse_grad = lax.dynamic_index_in_dim(coarse_rows, member // halves, 1, keepdims=False)
    hidden_delta = cotangent.astype(jnp.float32) + jnp.dot(
        assign_float,
        pooled_delta,
        precision=lax.Precision.HIGH,
        preferred_element_type=jnp.float32,
    )
    update_delta = (hidden_delta * silu_slope(update_pre)).astype(jnp.bfloat16)
    aggregated_delta = times_transposed(update_delta, w_second).astype(jnp.bfloat16)
    message_grad = transposed_times(summed_scaled, aggregated_delta)
    message_part = scatter_sum(message_grad.reshape(-1, across_count, chunk), "across", 1)
    grad_pieces = jnp.concatenate([message_part, coarse_grad], axis=0)
    weight_grads = scatter_sum(grad_pieces, "along")
    return (hidden_two.astype(jnp.bfloat16), weight_grads)


def solution(mesh):
    return jax.shard_map(
        local,
        mesh=mesh,
        in_specs=(
            P(("along", "across"), None),
            P(("along", "across"), None, None, None),
            P(("along", "across"), None),
            P(("along", "across")),
            P(("along", "across")),
            P(("along", "across")),
            P(),
            P(),
            P(),
            P(("along", "across"), None),
        ),
        out_specs=(P(("along", "across"), None), P(("along", "across"))),
        check_vma=False,
    )
```

```python
import jax
import jax.numpy as jnp
from jax import lax
from jax.sharding import PartitionSpec as P

NC_DEV = 4


eps = 1e-05


def scatter_sum(pieces, axes, dim=0):
    return lax.all_to_all(pieces, axes, dim, dim, tiled=False).sum(dim)


def all_sum(values, axis):
    count = lax.axis_size(axis)
    width = values.shape[-1]
    mine = scatter_sum(values.reshape(count, -1, width), axis)
    gathered = lax.all_to_all(jnp.broadcast_to(mine, (count,) + mine.shape), axis, 0, 0, tiled=False)
    return gathered.reshape(values.shape)


def neighbour_tiles(tile):
    tiles = []
    for axis in ("along", "across"):
        count = lax.axis_size(axis)
        forward = [(i, i + 1) for i in range(count - 1)]
        backward = [(i + 1, i) for i in range(count - 1)]
        tiles.append(lax.ppermute(tile, axis, forward))
        tiles.append(lax.ppermute(tile, axis, backward))
    return jnp.stack(tiles)


def row_sums(values, precision=None):
    ones = jnp.ones((values.shape[-1], 128), values.dtype)
    return jnp.dot(values, ones, precision=precision, preferred_element_type=jnp.float32)


def normalize_rows(features):
    width = features.shape[-1]
    repeat = width // 128
    mean = row_sums(features) / width
    center = features.astype(jnp.float32) - jnp.tile(mean, (1, repeat))
    variance = row_sums(center * center, lax.Precision.HIGH) / width
    inverse = lax.rsqrt(variance + eps)
    return center * jnp.tile(inverse, (1, repeat))


def split_bf16(values):
    high = lax.reduce_precision(values, exponent_bits=8, mantissa_bits=7)
    return high.astype(jnp.bfloat16), (values - high).astype(jnp.bfloat16)


def one_hot_times(one_hot, values, contract):
    high, low = split_bf16(values)
    dims = (((contract,), (0,)), ((), ()))
    return lax.dot_general(one_hot, high, dims, preferred_element_type=jnp.float32) + lax.dot_general(
        one_hot, low, dims, preferred_element_type=jnp.float32
    )


def normalize(values):
    center = values - jnp.mean(values, axis=-1, keepdims=True)
    inverse = lax.rsqrt(jnp.mean(center * center, axis=-1, keepdims=True) + eps)
    return (center * inverse, inverse)


def silu_slope(values):
    logistic = jax.nn.sigmoid(values)
    return logistic * (1.0 + values * (1.0 - logistic))


def transposed_times(operand, second, precision=None):
    return lax.dot_general(
        operand,
        second,
        (((0,), (0,)), ((), ())),
        precision=precision,
        preferred_element_type=jnp.float32,
    )


def times_transposed(operand, second):
    return lax.dot_general(
        operand, second, (((1,), (1,)), ((), ())), preferred_element_type=jnp.float32
    )


def coarse_forward(pooled, w_coarse):
    coarse_norm, inverse = normalize(pooled)
    coarse = coarse_norm.astype(jnp.bfloat16)
    coarse_pre = jnp.dot(coarse, w_coarse, preferred_element_type=jnp.float32)
    return (coarse_norm, inverse, coarse, coarse_pre, jax.nn.silu(coarse_pre).astype(jnp.bfloat16))


def coarse_backward(coarse_cot, coarse_norm, inverse, coarse_pre, w_coarse):
    coarse_delta = (coarse_cot * silu_slope(coarse_pre)).astype(jnp.bfloat16)
    coarse_back = times_transposed(coarse_delta, w_coarse)
    mean_one = jnp.mean(coarse_back, axis=-1, keepdims=True)
    mean_two = jnp.mean(coarse_back * coarse_norm, axis=-1, keepdims=True)
    return (coarse_delta, inverse * (coarse_back - mean_one - coarse_norm * mean_two))


def local(
    features,
    adj_tiles,
    adj_index,
    adj_count,
    bnd_index,
    pool_index,
    w_msg,
    w_update,
    w_coarse,
    cotangent,
):
    feature_count = features.shape[1]
    blocks = adj_tiles.shape[0]
    slot_count = adj_tiles.shape[1]
    tile_rows = adj_tiles.shape[2]
    inputs = features.astype(jnp.float32)
    normed = normalize_rows(features)
    scaled = normed.astype(jnp.bfloat16)
    node_count = scaled.shape[0]
    pick = (bnd_index[:, None] == jnp.arange(node_count)[None, :]).astype(jnp.bfloat16)
    rim_rows = jnp.dot(pick, scaled, preferred_element_type=jnp.float32).astype(jnp.bfloat16)
    halo_tiles = neighbour_tiles(rim_rows)
    sources = jnp.concatenate(
        [scaled.reshape(blocks, tile_rows, feature_count), halo_tiles], axis=0
    )
    live_slots = jnp.arange(slot_count)[None, :] < adj_count[:, None]
    masked_tiles = jnp.where(live_slots[:, :, None, None], adj_tiles, jnp.zeros((), jnp.bfloat16))
    summed = jnp.einsum(
        "bkij,bkjh->bih", masked_tiles, sources[adj_index], preferred_element_type=jnp.float32
    ).reshape(-1, feature_count)
    summed_high = lax.reduce_precision(summed, exponent_bits=8, mantissa_bits=7)
    summed_scaled = summed_high.astype(jnp.bfloat16)
    summed_low = (summed - summed_high).astype(jnp.bfloat16)
    aggregated = (
        jnp.dot(summed_scaled, w_msg, preferred_element_type=jnp.float32)
        + jnp.dot(summed_low, w_msg, preferred_element_type=jnp.float32)
    ).astype(jnp.bfloat16)
    w_first = w_update[:feature_count]
    w_second = w_update[feature_count:]
    update_pre = jnp.dot(scaled, w_first, preferred_element_type=jnp.float32) + jnp.dot(
        aggregated, w_second, preferred_element_type=jnp.float32
    )
    hidden_one = inputs + jax.nn.silu(update_pre)
    coarse_count = NC_DEV * lax.axis_size("across")
    assign_float = (pool_index[:, None] == jnp.arange(coarse_count)[None, :]).astype(jnp.float32)
    assign_bits = assign_float.astype(jnp.bfloat16)
    pooled_part = one_hot_times(assign_bits, hidden_one, 0)
    cot_part = transposed_times(assign_bits, cotangent)
    pooled, coarse_cot = all_sum(jnp.stack([pooled_part, cot_part]), "across")
    coarse_norm, inverse, coarse, coarse_pre, coarse_out = coarse_forward(pooled, w_coarse)
    hidden_two = hidden_one + jnp.dot(assign_bits, coarse_out, preferred_element_type=jnp.float32)
    coarse_delta, pooled_delta = coarse_backward(
        coarse_cot, coarse_norm, inverse, coarse_pre, w_coarse
    )
    along_count = lax.axis_size("along")
    across_count = lax.axis_size("across")
    chunk = (feature_count * feature_count) // (along_count * across_count // 2)
    halves = feature_count // chunk
    rows_per_step = across_count // halves
    member = lax.axis_index("across")
    picked_cols = lax.dynamic_slice_in_dim(coarse_delta, (member % halves) * chunk, chunk, 1)
    coarse_rows = transposed_times(coarse, picked_cols).reshape(-1, rows_per_step, chunk)
    coarse_grad = lax.dynamic_index_in_dim(coarse_rows, member // halves, 1, keepdims=False)
    hidden_delta = cotangent.astype(jnp.float32) + one_hot_times(assign_bits, pooled_delta, 1)
    update_delta = (hidden_delta * silu_slope(update_pre)).astype(jnp.bfloat16)
    aggregated_delta = times_transposed(update_delta, w_second).astype(jnp.bfloat16)
    message_grad = transposed_times(summed_scaled, aggregated_delta)
    message_part = scatter_sum(message_grad.reshape(-1, across_count, chunk), "across", 1)
    grad_pieces = jnp.concatenate([message_part, coarse_grad], axis=0)
    weight_grads = scatter_sum(grad_pieces, "along")
    return (hidden_two.astype(jnp.bfloat16), weight_grads)


def solution(mesh):
    return jax.shard_map(
        local,
        mesh=mesh,
        in_specs=(
            P(("along", "across"), None),
            P(("along", "across"), None, None, None),
            P(("along", "across"), None),
            P(("along", "across")),
            P(("along", "across")),
            P(("along", "across")),
            P(),
            P(),
            P(),
            P(("along", "across"), None),
        ),
        out_specs=(P(("along", "across"), None), P(("along", "across"))),
        check_vma=False,
    )
```

```python
import jax
import jax.numpy as jnp
from jax import lax
from jax.sharding import PartitionSpec as P

NC_DEV = 4


eps = 1e-05


def scatter_sum(pieces, axes, dim=0):
    return lax.all_to_all(pieces, axes, dim, dim, tiled=False).sum(dim)


def all_sum(values, axis):
    count = lax.axis_size(axis)
    width = values.shape[-1]
    mine = scatter_sum(values.reshape(count, -1, width), axis)
    gathered = lax.all_to_all(jnp.broadcast_to(mine, (count,) + mine.shape), axis, 0, 0, tiled=False)
    return gathered.reshape(values.shape)


def neighbour_tiles(tile):
    tiles = []
    for axis in ("along", "across"):
        count = lax.axis_size(axis)
        forward = [(i, i + 1) for i in range(count - 1)]
        backward = [(i + 1, i) for i in range(count - 1)]
        tiles.append(lax.ppermute(tile, axis, forward))
        tiles.append(lax.ppermute(tile, axis, backward))
    return jnp.stack(tiles)


def row_sums(values, precision=None):
    ones = jnp.ones((values.shape[-1], 128), values.dtype)
    return jnp.dot(values, ones, precision=precision, preferred_element_type=jnp.float32)


def normalize_rows(features):
    width = features.shape[-1]
    repeat = width // 128
    mean = row_sums(features) / width
    center = features.astype(jnp.float32) - jnp.tile(mean, (1, repeat))
    variance = row_sums(center * center, lax.Precision.HIGH) / width
    inverse = lax.rsqrt(variance + eps)
    return center * jnp.tile(inverse, (1, repeat))


def normalize(values):
    center = values - jnp.mean(values, axis=-1, keepdims=True)
    inverse = lax.rsqrt(jnp.mean(center * center, axis=-1, keepdims=True) + eps)
    return (center * inverse, inverse)


def silu_slope(values):
    logistic = jax.nn.sigmoid(values)
    return logistic * (1.0 + values * (1.0 - logistic))


def transposed_times(operand, second, precision=None):
    return lax.dot_general(
        operand,
        second,
        (((0,), (0,)), ((), ())),
        precision=precision,
        preferred_element_type=jnp.float32,
    )


def times_transposed(operand, second):
    return lax.dot_general(
        operand, second, (((1,), (1,)), ((), ())), preferred_element_type=jnp.float32
    )


def coarse_forward(pooled, w_coarse):
    coarse_norm, inverse = normalize(pooled)
    coarse = coarse_norm.astype(jnp.bfloat16)
    coarse_pre = jnp.dot(coarse, w_coarse, preferred_element_type=jnp.float32)
    return (coarse_norm, inverse, coarse, coarse_pre, jax.nn.silu(coarse_pre).astype(jnp.bfloat16))


def coarse_backward(coarse_cot, coarse_norm, inverse, coarse_pre, w_coarse):
    coarse_delta = (coarse_cot * silu_slope(coarse_pre)).astype(jnp.bfloat16)
    coarse_back = times_transposed(coarse_delta, w_coarse)
    mean_one = jnp.mean(coarse_back, axis=-1, keepdims=True)
    mean_two = jnp.mean(coarse_back * coarse_norm, axis=-1, keepdims=True)
    return (coarse_delta, inverse * (coarse_back - mean_one - coarse_norm * mean_two))


def local(
    features,
    adj_tiles,
    adj_index,
    adj_count,
    bnd_index,
    pool_index,
    w_msg,
    w_update,
    w_coarse,
    cotangent,
):
    feature_count = features.shape[1]
    blocks = adj_tiles.shape[0]
    slot_count = adj_tiles.shape[1]
    tile_rows = adj_tiles.shape[2]
    inputs = features.astype(jnp.float32)
    normed = normalize_rows(features)
    scaled = normed.astype(jnp.bfloat16)
    node_count = scaled.shape[0]
    pick = (bnd_index[:, None] == jnp.arange(node_count)[None, :]).astype(jnp.bfloat16)
    rim_rows = jnp.dot(pick, scaled, preferred_element_type=jnp.float32).astype(jnp.bfloat16)
    halo_tiles = neighbour_tiles(rim_rows)
    sources = jnp.concatenate(
        [scaled.reshape(blocks, tile_rows, feature_count), halo_tiles], axis=0
    )
    live_slots = jnp.arange(slot_count)[None, :] < adj_count[:, None]
    masked_tiles = jnp.where(live_slots[:, :, None, None], adj_tiles, jnp.zeros((), jnp.bfloat16))
    summed = jnp.einsum(
        "bkij,bkjh->bih", masked_tiles, sources[adj_index], preferred_element_type=jnp.float32
    ).reshape(-1, feature_count)
    summed_high = lax.reduce_precision(summed, exponent_bits=8, mantissa_bits=7)
    summed_scaled = summed_high.astype(jnp.bfloat16)
    summed_low = (summed - summed_high).astype(jnp.bfloat16)
    aggregated = (
        jnp.dot(summed_scaled, w_msg, preferred_element_type=jnp.float32)
        + jnp.dot(summed_low, w_msg, preferred_element_type=jnp.float32)
    ).astype(jnp.bfloat16)
    w_first = w_update[:feature_count]
    w_second = w_update[feature_count:]
    update_pre = jnp.dot(scaled, w_first, preferred_element_type=jnp.float32) + jnp.dot(
        aggregated, w_second, preferred_element_type=jnp.float32
    )
    hidden_one = inputs + jax.nn.silu(update_pre)
    coarse_count = NC_DEV * lax.axis_size("across")
    assign_float = (pool_index[:, None] == jnp.arange(coarse_count)[None, :]).astype(jnp.float32)
    assign_bits = assign_float.astype(jnp.bfloat16)
    members = (jnp.arange(coarse_count)[:, None] == pool_index[None, :]).astype(jnp.float32)
    pooled_part = jnp.dot(members, hidden_one, precision=lax.Precision.HIGH, preferred_element_type=jnp.float32)
    cot_part = jnp.dot(members.astype(jnp.bfloat16), cotangent, preferred_element_type=jnp.float32)
    pooled, coarse_cot = all_sum(jnp.stack([pooled_part, cot_part]), "across")
    coarse_norm, inverse, coarse, coarse_pre, coarse_out = coarse_forward(pooled, w_coarse)
    hidden_two = hidden_one + jnp.dot(assign_bits, coarse_out, preferred_element_type=jnp.float32)
    coarse_delta, pooled_delta = coarse_backward(
        coarse_cot, coarse_norm, inverse, coarse_pre, w_coarse
    )
    along_count = lax.axis_size("along")
    across_count = lax.axis_size("across")
    chunk = (feature_count * feature_count) // (along_count * across_count // 2)
    halves = feature_count // chunk
    rows_per_step = across_count // halves
    member = lax.axis_index("across")
    picked_cols = lax.dynamic_slice_in_dim(coarse_delta, (member % halves) * chunk, chunk, 1)
    coarse_rows = transposed_times(coarse, picked_cols).reshape(-1, rows_per_step, chunk)
    coarse_grad = lax.dynamic_index_in_dim(coarse_rows, member // halves, 1, keepdims=False)
    hidden_delta = cotangent.astype(jnp.float32) + jnp.dot(
        assign_float,
        pooled_delta,
        precision=lax.Precision.HIGH,
        preferred_element_type=jnp.float32,
    )
    update_delta = (hidden_delta * silu_slope(update_pre)).astype(jnp.bfloat16)
    aggregated_delta = times_transposed(update_delta, w_second).astype(jnp.bfloat16)
    message_grad = transposed_times(summed_scaled, aggregated_delta)
    message_part = scatter_sum(message_grad.reshape(-1, across_count, chunk), "across", 1)
    grad_pieces = jnp.concatenate([message_part, coarse_grad], axis=0)
    weight_grads = scatter_sum(grad_pieces, "along")
    return (hidden_two.astype(jnp.bfloat16), weight_grads)


def solution(mesh):
    return jax.shard_map(
        local,
        mesh=mesh,
        in_specs=(
            P(("along", "across"), None),
            P(("along", "across"), None, None, None),
            P(("along", "across"), None),
            P(("along", "across")),
            P(("along", "across")),
            P(("along", "across")),
            P(),
            P(),
            P(),
            P(("along", "across"), None),
        ),
        out_specs=(P(("along", "across"), None), P(("along", "across"))),
        check_vma=False,
    )
```
